32 devices in a mesh: basin: 2 (over y), tx: 8 (over z, x), ty: 2 (over core).
Axes of the slice: x: 2, y: 2, z: 4, core: 2. Of those that a mesh axis runs over, the one named last changes fastest.
Arguments:
- jac_blocks: bfloat16 [896, 128, 128], P(('basin', 'tx', 'ty')), parts along dimension 0, may hold values from -0.1875 to 0.1875
- jac_rows: int32 [896], P(('basin', 'tx', 'ty')), parts along dimension 0, may hold values from 0 to 11, as said below
- jac_cols: int32 [896], P(('basin', 'tx', 'ty')), parts along dimension 0, may hold values from 0 to 3
- landing: int32 [256], P(('basin', 'tx', 'ty')), parts along dimension 0, may hold values from 0 to 3
- covariance_root: bfloat16 [16384, 512], P(('basin', 'tx', 'ty')), parts along dimension 0
Outputs:
- rescaled_orthogonal_root: bfloat16 [16384, 512], P(('basin', 'tx', 'ty')), parts along dimension 0
- r_factor: float32 [1024, 512], P('basin'), parts along dimension 0
The draws below stay inside these ranges and needn't reach their ends.
There are 2 independent parts, one for each index of `basin`. The reference program is written for one: setup_inputs(seed, part) draws one part's arguments, and reference() takes and returns one part's arrays. A program takes and returns all parts, laid end to end along the dimension named above; each array names one. Nothing has to cross between parts.
Inputs may be any that keep to these rules, and one draw needn't show every extreme that they name: `jac_rows`: in each device's list of 28 blocks every row slot from 0 to 11 appears at least once.
All inputs are finite; a program needn't handle non-finite values.
Results may differ from the reference program's by a relative error of at most 0.001.
Values sent between devices are 32-bit elements; how exact they have to be, the bound alone decides.
No kernel may reach another device: no remote copies, remote signals or barrier semaphores. Data moves between devices by JAX's collectives and lax.ppermute only.
A program may use at most 64 MiB of HBM per device.

```python
import math
import jax
import jax.numpy as jnp
from jax import lax

ROOT_PATTERNS = 512
BS = 128
RIM = 2
BLK_DEV = 4
NNZ_DEV = 28
CATCHMENT_POINTS = 8192
BLOCKS_ALL = 448
LANDS = 128
N_TX = 8
N_TY = 2


def draw_jac_rows(key, part):
    slot_count = BLK_DEV + 4 * RIM

    def single(subkey):
        first, second, third = jax.random.split(subkey, 3)
        cover = jax.random.permutation(first, slot_count).astype(jnp.int32)
        extra = jax.random.randint(second, (NNZ_DEV - slot_count,), 0, slot_count).astype(jnp.int32)
        return jax.random.permutation(third, jnp.concatenate([cover, extra])).astype(jnp.int32)
    subkeys = jax.random.split(jax.random.fold_in(key, 11), N_TX * N_TY)
    return jax.vmap(single)(subkeys).reshape(-1).astype(jnp.int32)


def draw_covariance_root(key, part):
    first, second, third, fourth, fifth = jax.random.split(jax.random.fold_in(key, 7), 5)
    shape = (CATCHMENT_POINTS, ROOT_PATTERNS)
    base = jax.random.normal(first, shape, jnp.float32)
    shared = jax.random.normal(fourth, (CATCHMENT_POINTS, 4), jnp.float32)
    mixing = 0.5 * jax.random.normal(fifth, (4, ROOT_PATTERNS), jnp.float32)
    row_lo = math.log(0.3)
    row_hi = math.log(3.0)
    common = shared[:, 0:1] * mixing[0:1, :]
    common = common + shared[:, 1:2] * mixing[1:2, :]
    common = common + shared[:, 2:3] * mixing[2:3, :]
    common = common + shared[:, 3:4] * mixing[3:4, :]
    mixed = base + common
    position = jnp.arange(CATCHMENT_POINTS, dtype=jnp.float32)[:, None] / CATCHMENT_POINTS
    row_scale = jnp.exp(jax.random.uniform(second, (CATCHMENT_POINTS, 1), jnp.float32, row_lo, row_hi)) * jnp.power(3.0, position)
    col_scale = jnp.exp(jax.random.uniform(third, (1, ROOT_PATTERNS), jnp.float32, math.log(0.3), math.log(3.0)))
    return (mixed * row_scale * col_scale).astype(jnp.bfloat16)


def touch_ends(values, own_key, smallest, largest):
    longest = values.shape.index(max(values.shape))
    spots = []
    for shift in (0, 1):
        where = [jax.random.randint(jax.random.fold_in(own_key, axis), (), 0, length) for axis, length in enumerate(values.shape)]
        where[longest] = (where[longest] + shift) % values.shape[longest]
        spots.append(tuple(where))
    return values.at[spots[0]].set(smallest).at[spots[1]].set(largest)


def block_scale(own_key, dims, shards, low, top_value):
    level, own = 1.0, jax.random.fold_in(own_key, 6)
    for dim, blocks in shards:
        steps = jnp.exp(jax.random.uniform(jax.random.fold_in(own, dim), (blocks,), jnp.float32, low / len(shards), top_value / len(shards)))
        level = level * jnp.repeat(steps, dims[dim] // blocks).reshape([-1 if axis == dim else 1 for axis in range(len(dims))])
    return level


def centred(rng, shape, deviation, reach, cuts=(), kind=jnp.bfloat16):
    values = jax.random.normal(rng, shape, jnp.float32) * deviation
    if len(cuts) > 0:
        values = block_scale(rng, shape, cuts, -0.22, 0.18) * values
    return jnp.clip(values, min=-reach, max=reach).astype(kind)


def setup_inputs(seed: int = 0, part: int = 0) -> dict:
    key_of = jax.random.split(jax.random.key(seed), 6)
    part_keys = jax.random.split(jax.random.fold_in(key_of[5], part), 6)
    return {
        "jac_blocks": centred(part_keys[0], (BLOCKS_ALL, BS, BS), (4 * BS * NNZ_DEV // (BLK_DEV + 4 * RIM)) ** -0.5, 0.1875, ((0, 16),)),
        "jac_rows": draw_jac_rows(jax.random.fold_in(jax.random.fold_in(key_of[5], part), 71), part),
        "jac_cols": touch_ends(jax.random.randint(part_keys[2], (BLOCKS_ALL,), 0, BLK_DEV), jax.random.fold_in(part_keys[2], 1), 0, BLK_DEV - 1).astype(jnp.int32),
        "landing": touch_ends(jax.random.randint(part_keys[3], (LANDS,), 0, BLK_DEV), jax.random.fold_in(part_keys[3], 1), 0, BLK_DEV - 1).astype(jnp.int32),
        "covariance_root": draw_covariance_root(jax.random.fold_in(jax.random.fold_in(key_of[5], part), 71), part),
    }


def device_partial(args):
    jac, state_rows, cols, lfac = args
    blocks = lfac.reshape(BLK_DEV, BS, ROOT_PATTERNS)
    picked = jnp.take(blocks, cols.astype(jnp.int32), axis=0)
    product = jnp.einsum('nij,njq->niq', jac.astype(jnp.float32), picked.astype(jnp.float32), precision=lax.Precision.HIGHEST)
    slots = jnp.arange(BLK_DEV + 4 * RIM, dtype=jnp.int32)
    onehot = (state_rows.astype(jnp.int32)[None, :] == slots[:, None]).astype(jnp.float32)
    return jnp.dot(onehot.astype(jnp.float32), product.reshape(NNZ_DEV, BS * ROOT_PATTERNS).astype(jnp.float32), precision=lax.Precision.HIGHEST, preferred_element_type=jnp.float32)

def reference(jac_blocks, jac_rows, jac_cols, landing, covariance_root):
    devs = N_TX * N_TY
    width = BS * ROOT_PATTERNS
    partial_value = lax.map(device_partial, (jac_blocks.reshape(devs, NNZ_DEV, BS, BS), jac_rows.reshape(devs, NNZ_DEV), jac_cols.reshape(devs, NNZ_DEV), covariance_root.reshape(devs, BLK_DEV * BS, ROOT_PATTERNS)))
    partial_value = partial_value.reshape(N_TX, N_TY, BLK_DEV + 4 * RIM, width)
    diagonal_submatrix = partial_value[:, :, :BLK_DEV]
    outgoing = partial_value[:, :, BLK_DEV:].reshape(N_TX, N_TY, 4, RIM, width)
    zero_x = jnp.zeros((1, N_TY, RIM, width), jnp.float32)
    zero_y = jnp.zeros((N_TX, 1, RIM, width), jnp.float32)
    from_next_x = jnp.concatenate([outgoing[1:, :, 0], zero_x], axis=0)
    from_prev_x = jnp.concatenate([zero_x, outgoing[:-1, :, 1]], axis=0)
    from_next_y = jnp.concatenate([outgoing[:, 1:, 2], zero_y], axis=1)
    from_prev_y = jnp.concatenate([zero_y, outgoing[:, :-1, 3]], axis=1)
    incoming = jnp.stack([from_next_x, from_prev_x, from_next_y, from_prev_y], axis=2).reshape(N_TX, N_TY, 4 * RIM, width)
    lands = landing.astype(jnp.int32).reshape(N_TX, N_TY, 4 * RIM)
    targets = jnp.arange(BLK_DEV, dtype=jnp.int32)
    onehot = (lands[:, :, None, :] == targets[None, None, :, None]).astype(jnp.float32)
    contribution_pieces = jnp.einsum('abke,abex->abkx', onehot, incoming, precision=lax.Precision.HIGHEST)
    predicted_root = covariance_root.astype(jnp.float32) + (diagonal_submatrix + contribution_pieces).reshape(CATCHMENT_POINTS, ROOT_PATTERNS)
    inner_products_table = jnp.dot(predicted_root.T.astype(jnp.float32), predicted_root.astype(jnp.float32), precision=lax.Precision.HIGHEST, preferred_element_type=jnp.float32) / CATCHMENT_POINTS
    cholesky_bottom_triangle = jnp.linalg.cholesky(inner_products_table)
    rescaled_orthogonal_root = lax.linalg.triangular_solve(cholesky_bottom_triangle, predicted_root, left_side=False, lower=True, transpose_a=True)
    return (rescaled_orthogonal_root.astype(jnp.bfloat16), cholesky_bottom_triangle.T)
```

```python
import jax
import jax.numpy as jnp
from jax import lax
from jax.sharding import PartitionSpec as P


def shifted(block, axis, distance):
    devices = range(lax.axis_size(axis))
    route = [(i - distance, i) for i in devices if i - distance in devices]
    return lax.ppermute(block, axis, route)


def doubling_sum(block, axis):
    size = lax.axis_size(axis)
    distance = 1
    while distance < size:
        route = [(i, i ^ distance) for i in range(size)]
        block = block + lax.ppermute(block, axis, route)
        distance *= 2
    return block


def reduce_tiles(tiles):
    count = tiles.shape[0]
    if lax.axis_size("ty") != 2 or count % 2:
        return doubling_sum(doubling_sum(tiles, "tx"), "ty")
    half = count // 2
    side = lax.axis_index("ty")
    swap = [(0, 1), (1, 0)]
    sent = lax.dynamic_slice_in_dim(tiles, (1 - side) * half, half, axis=0)
    kept = lax.dynamic_slice_in_dim(tiles, side * half, half, axis=0)
    kept = kept + lax.ppermute(sent, "ty", swap)
    kept = doubling_sum(kept, "tx")
    other = lax.ppermute(kept, "ty", swap)
    return jnp.where(side == 0, jnp.concatenate([kept, other]), jnp.concatenate([other, kept]))


def per_device(jac_blocks, jac_rows, jac_cols, landing, covariance_root):
    nnz, block, _ = jac_blocks.shape
    state_rows, mode_columns = covariance_root.shape
    nblk = state_rows // block
    rim = landing.shape[0] // 4
    slot_count = nblk + 4 * rim
    width = block * mode_columns
    blocks = covariance_root.reshape(nblk, block, mode_columns)
    picked = jnp.take(blocks, jac_cols, axis=0)
    product = jnp.einsum("nij,njq->niq", jac_blocks, picked, preferred_element_type=jnp.float32)
    slot_ids = jnp.arange(slot_count, dtype=jnp.int32)
    slot_table = (jac_rows[None, :] == slot_ids[:, None]).astype(jnp.float32)
    partial_value = jnp.dot(
        slot_table,
        product.reshape(nnz, width),
        precision=lax.Precision.HIGHEST,
        preferred_element_type=jnp.float32,
    )
    diagonal_submatrix = partial_value[:nblk]
    outgoing = partial_value[nblk:].reshape(4, rim, width)
    from_next_x = shifted(outgoing[0], "tx", -1)
    from_prev_x = shifted(outgoing[1], "tx", 1)
    from_next_y = shifted(outgoing[2], "ty", -1)
    from_prev_y = shifted(outgoing[3], "ty", 1)
    incoming = jnp.stack([from_next_x, from_prev_x, from_next_y, from_prev_y], axis=0).reshape(
        4 * rim, width
    )
    targets = jnp.arange(nblk, dtype=jnp.int32)
    land_table = (landing[None, :] == targets[:, None]).astype(jnp.float32)
    contribution_pieces = jnp.dot(
        land_table, incoming, precision=lax.Precision.HIGHEST, preferred_element_type=jnp.float32
    )
    predicted_root = covariance_root.astype(jnp.float32) + (
        diagonal_submatrix + contribution_pieces
    ).reshape(state_rows, mode_columns)
    local_gram = lax.dot_general(
        predicted_root,
        predicted_root,
        (((0,), (0,)), ((), ())),
        precision=lax.Precision.HIGHEST,
        preferred_element_type=jnp.float32,
    )
    total_rows = state_rows * lax.axis_size("tx") * lax.axis_size("ty")
    tiles = mode_columns // block
    upper_list = []
    for first in range(tiles):
        for second in range(first, tiles):
            upper_list.append(
                local_gram[
                    first * block : (first + 1) * block, second * block : (second + 1) * block
                ]
            )
    upper_sum = reduce_tiles(jnp.stack(upper_list, axis=0))
    position = {}
    counter = 0
    for first in range(tiles):
        for second in range(first, tiles):
            position[first, second] = counter
            counter = counter + 1
    band_rows = []
    for first in range(tiles):
        pieces = []
        for second in range(tiles):
            if first <= second:
                pieces.append(upper_sum[position[first, second]])
            else:
                pieces.append(upper_sum[position[second, first]].T)
        band_rows.append(jnp.concatenate(pieces, axis=1))
    summed = jnp.concatenate(band_rows, axis=0)
    inner_products_table = summed / total_rows
    cholesky_bottom_triangle = jnp.linalg.cholesky(inner_products_table)
    rescaled_orthogonal_root = lax.linalg.triangular_solve(
        cholesky_bottom_triangle, predicted_root, left_side=False, lower=True, transpose_a=True
    )
    return (rescaled_orthogonal_root.astype(jnp.bfloat16), cholesky_bottom_triangle.T)


def solution(mesh):
    placed = (
        P(("basin", "tx", "ty"), None, None),
        P(("basin", "tx", "ty")),
        P(("basin", "tx", "ty")),
        P(("basin", "tx", "ty")),
        P(("basin", "tx", "ty"), None),
    )
    return jax.shard_map(
        per_device,
        mesh=mesh,
        in_specs=placed,
        out_specs=(P(("basin", "tx", "ty"), None), P("basin", None)),
        check_vma=False,
    )
```

```python
import jax
import jax.numpy as jnp
from jax import lax
from jax.experimental import pallas as pl
from jax.experimental.pallas import tpu as pltpu
from jax.sharding import PartitionSpec as P

HI = lax.Precision.HIGHEST


def factor_kernel(g_ref, f_ref, x_ref, u_ref, w_ref, inv_ref, xs_ref):
    n = g_ref.shape[0]
    b = inv_ref.shape[1]
    nb = n // b
    w_ref[...] = g_ref[...]
    u_ref[...] = jnp.zeros(u_ref.shape, jnp.float32)
    lane = lax.broadcasted_iota(jnp.int32, (1, b), 1)
    rows = lax.broadcasted_iota(jnp.int32, (b, 1), 0)
    eye = jnp.where(lax.broadcasted_iota(jnp.int32, (b, b), 0) == lax.broadcasted_iota(jnp.int32, (b, b), 1), 1.0, 0.0)
    for k in range(nb):
        o = k * b
        inv_ref[k] = eye
        for j in range(b):
            r = w_ref[o + j:o + j + 1, o:o + b]
            rs = lax.rsqrt(r[:, j:j + 1])
            u = jnp.where(lane >= j, r, 0.0) * rs
            u_ref[o + j:o + j + 1, o:o + b] = u
            brow = inv_ref[k, j:j + 1, :] * rs
            inv_ref[k, j:j + 1, :] = brow
            if j == b - 1:
                break
            s = (j + 1) // 8 * 8
            v = w_ref[o + s:o + b, o + j:o + j + 1] * rs
            v = jnp.where(rows[s:] > j, v, 0.0)
            w_ref[o + s:o + b, o:o + b] = w_ref[o + s:o + b, o:o + b] - v * u
            inv_ref[k, s:, :] = inv_ref[k, s:, :] - v * brow
        if k < nb - 1:
            e = o + b
            panel = jnp.dot(inv_ref[k], w_ref[o:e, e:], precision=HI, preferred_element_type=jnp.float32)
            u_ref[o:e, e:] = panel
            w_ref[e:, e:] = w_ref[e:, e:] - lax.dot_general(
                panel, panel, (((0,), (0,)), ((), ())), precision=HI, preferred_element_type=jnp.float32)
    for k in range(nb):
        o = k * b
        y = f_ref[:, o:o + b]
        if k > 0:
            y = y - jnp.dot(xs_ref[:, :o], u_ref[:o, o:o + b], precision=HI, preferred_element_type=jnp.float32)
        xs_ref[:, o:o + b] = lax.dot_general(
            y, inv_ref[k], (((1,), (1,)), ((), ())), precision=HI, preferred_element_type=jnp.float32)
    x_ref[...] = xs_ref[...].astype(x_ref.dtype)


def factor_solve(gram, forecast, block=128):
    n = gram.shape[0]
    m = forecast.shape[0]
    vmem = pl.BlockSpec(memory_space=pltpu.VMEM)
    return pl.pallas_call(
        factor_kernel,
        out_shape=(jax.ShapeDtypeStruct((m, n), jnp.bfloat16), jax.ShapeDtypeStruct((n, n), jnp.float32)),
        in_specs=[vmem, vmem],
        out_specs=(vmem, vmem),
        scratch_shapes=[
            pltpu.VMEM((n, n), jnp.float32),
            pltpu.VMEM((n // block, block, block), jnp.float32),
            pltpu.VMEM((m, n), jnp.float32),
        ],
    )(gram, forecast)


def shifted(block, axis, distance):
    devices = range(lax.axis_size(axis))
    route = [(i - distance, i) for i in devices if i - distance in devices]
    return lax.ppermute(block, axis, route)


def doubling_sum(block, axis):
    size = lax.axis_size(axis)
    distance = 1
    while distance < size:
        route = [(i, i ^ distance) for i in range(size)]
        block = block + lax.ppermute(block, axis, route)
        distance *= 2
    return block


def reduce_tiles(tiles):
    count = tiles.shape[0]
    if lax.axis_size("ty") != 2 or count % 2:
        return doubling_sum(doubling_sum(tiles, "tx"), "ty")
    half = count // 2
    side = lax.axis_index("ty")
    swap = [(0, 1), (1, 0)]
    sent = lax.dynamic_slice_in_dim(tiles, (1 - side) * half, half, axis=0)
    kept = lax.dynamic_slice_in_dim(tiles, side * half, half, axis=0)
    kept = kept + lax.ppermute(sent, "ty", swap)
    kept = doubling_sum(kept, "tx")
    other = lax.ppermute(kept, "ty", swap)
    return jnp.where(side == 0, jnp.concatenate([kept, other]), jnp.concatenate([other, kept]))


def per_device(jac_blocks, jac_rows, jac_cols, landing, covariance_root):
    nnz, block, _ = jac_blocks.shape
    state_rows, mode_columns = covariance_root.shape
    nblk = state_rows // block
    rim = landing.shape[0] // 4
    slot_count = nblk + 4 * rim
    width = block * mode_columns
    blocks = covariance_root.reshape(nblk, block, mode_columns)
    picked = jnp.take(blocks, jac_cols, axis=0)
    product = jnp.einsum("nij,njq->niq", jac_blocks, picked, preferred_element_type=jnp.float32)
    slot_ids = jnp.arange(slot_count, dtype=jnp.int32)
    slot_table = (jac_rows[None, :] == slot_ids[:, None]).astype(jnp.float32)
    partial_value = jnp.dot(
        slot_table,
        product.reshape(nnz, width),
        precision=lax.Precision.HIGHEST,
        preferred_element_type=jnp.float32,
    )
    diagonal_submatrix = partial_value[:nblk]
    outgoing = partial_value[nblk:].reshape(4, rim, width)
    from_next_x = shifted(outgoing[0], "tx", -1)
    from_prev_x = shifted(outgoing[1], "tx", 1)
    from_next_y = shifted(outgoing[2], "ty", -1)
    from_prev_y = shifted(outgoing[3], "ty", 1)
    incoming = jnp.stack([from_next_x, from_prev_x, from_next_y, from_prev_y], axis=0).reshape(
        4 * rim, width
    )
    targets = jnp.arange(nblk, dtype=jnp.int32)
    land_table = (landing[None, :] == targets[:, None]).astype(jnp.float32)
    contribution_pieces = jnp.dot(
        land_table, incoming, precision=lax.Precision.HIGHEST, preferred_element_type=jnp.float32
    )
    predicted_root = covariance_root.astype(jnp.float32) + (
        diagonal_submatrix + contribution_pieces
    ).reshape(state_rows, mode_columns)
    local_gram = lax.dot_general(
        predicted_root,
        predicted_root,
        (((0,), (0,)), ((), ())),
        precision=lax.Precision.HIGHEST,
        preferred_element_type=jnp.float32,
    )
    total_rows = state_rows * lax.axis_size("tx") * lax.axis_size("ty")
    tiles = mode_columns // block
    upper_list = []
    for first in range(tiles):
        for second in range(first, tiles):
            upper_list.append(
                local_gram[
                    first * block : (first + 1) * block, second * block : (second + 1) * block
                ]
            )
    upper_sum = reduce_tiles(jnp.stack(upper_list, axis=0))
    position = {}
    counter = 0
    for first in range(tiles):
        for second in range(first, tiles):
            position[first, second] = counter
            counter = counter + 1
    band_rows = []
    for first in range(tiles):
        pieces = []
        for second in range(tiles):
            if first <= second:
                pieces.append(upper_sum[position[first, second]])
            else:
                pieces.append(upper_sum[position[second, first]].T)
        band_rows.append(jnp.concatenate(pieces, axis=1))
    summed = jnp.concatenate(band_rows, axis=0)
    inner_products_table = summed / total_rows
    rescaled_orthogonal_root, r_factor = factor_solve(inner_products_table, predicted_root, block)
    return (rescaled_orthogonal_root, r_factor)


def solution(mesh):
    placed = (
        P(("basin", "tx", "ty"), None, None),
        P(("basin", "tx", "ty")),
        P(("basin", "tx", "ty")),
        P(("basin", "tx", "ty")),
        P(("basin", "tx", "ty"), None),
    )
    return jax.shard_map(
        per_device,
        mesh=mesh,
        in_specs=placed,
        out_specs=(P(("basin", "tx", "ty"), None), P("basin", None)),
        check_vma=False,
    )
```

```python
import jax
import jax.numpy as jnp
from jax import lax
from jax.experimental import pallas as pl
from jax.experimental.pallas import tpu as pltpu
from jax.sharding import PartitionSpec as P

HI = lax.Precision.HIGHEST


def factor_kernel(g_ref, f_ref, x_ref, u_ref, w_ref, inv_ref, xs_ref):
    n = g_ref.shape[0]
    b = inv_ref.shape[1]
    nb = n // b
    w_ref[...] = g_ref[...]
    u_ref[...] = jnp.zeros(u_ref.shape, jnp.float32)
    lane = lax.broadcasted_iota(jnp.int32, (1, b), 1)
    rows = lax.broadcasted_iota(jnp.int32, (b, 1), 0)
    eye = jnp.where(lax.broadcasted_iota(jnp.int32, (b, b), 0) == lax.broadcasted_iota(jnp.int32, (b, b), 1), 1.0, 0.0)
    for k in range(nb):
        o = k * b
        inv_ref[k] = eye
        for j in range(b):
            r = w_ref[o + j:o + j + 1, o:o + b]
            rs = lax.rsqrt(r[:, j:j + 1])
            u = jnp.where(lane >= j, r, 0.0) * rs
            u_ref[o + j:o + j + 1, o:o + b] = u
            brow = inv_ref[k, j:j + 1, :] * rs
            inv_ref[k, j:j + 1, :] = brow
            if j == b - 1:
                break
            s = (j + 1) // 8 * 8
            v = w_ref[o + s:o + b, o + j:o + j + 1] * rs
            v = jnp.where(rows[s:] > j, v, 0.0)
            w_ref[o + s:o + b, o:o + b] = w_ref[o + s:o + b, o:o + b] - v * u
            inv_ref[k, s:, :] = inv_ref[k, s:, :] - v * brow
        if k < nb - 1:
            e = o + b
            panel = jnp.dot(inv_ref[k], w_ref[o:e, e:], precision=HI, preferred_element_type=jnp.float32)
            u_ref[o:e, e:] = panel
            w_ref[e:, e:] = w_ref[e:, e:] - lax.dot_general(
                panel, panel, (((0,), (0,)), ((), ())), precision=HI, preferred_element_type=jnp.float32)
    for k in range(nb):
        o = k * b
        y = f_ref[:, o:o + b]
        if k > 0:
            y = y - jnp.dot(xs_ref[:, :o], u_ref[:o, o:o + b], precision=HI, preferred_element_type=jnp.float32)
        xs_ref[:, o:o + b] = lax.dot_general(
            y, inv_ref[k], (((1,), (1,)), ((), ())), precision=HI, preferred_element_type=jnp.float32)
    x_ref[...] = xs_ref[...].astype(x_ref.dtype)


def factor_solve(gram, forecast, block=128):
    n = gram.shape[0]
    m = forecast.shape[0]
    vmem = pl.BlockSpec(memory_space=pltpu.VMEM)
    return pl.pallas_call(
        factor_kernel,
        out_shape=(jax.ShapeDtypeStruct((m, n), jnp.bfloat16), jax.ShapeDtypeStruct((n, n), jnp.float32)),
        in_specs=[vmem, vmem],
        out_specs=(vmem, vmem),
        scratch_shapes=[
            pltpu.VMEM((n, n), jnp.float32),
            pltpu.VMEM((n // block, block, block), jnp.float32),
            pltpu.VMEM((m, n), jnp.float32),
        ],
    )(gram, forecast)


def shifted(block, axis, distance):
    devices = range(lax.axis_size(axis))
    route = [(i - distance, i) for i in devices if i - distance in devices]
    return lax.ppermute(block, axis, route)


def doubling_sum(block, axis):
    size = lax.axis_size(axis)
    distance = 1
    while distance < size:
        route = [(i, i ^ distance) for i in range(size)]
        block = block + lax.ppermute(block, axis, route)
        distance *= 2
    return block


def reduce_tiles(tiles):
    count = tiles.shape[0]
    if lax.axis_size("ty") != 2 or count % 2:
        return doubling_sum(doubling_sum(tiles, "tx"), "ty")
    half = count // 2
    side = lax.axis_index("ty")
    swap = [(0, 1), (1, 0)]
    sent = lax.dynamic_slice_in_dim(tiles, (1 - side) * half, half, axis=0)
    kept = lax.dynamic_slice_in_dim(tiles, side * half, half, axis=0)
    kept = kept + lax.ppermute(sent, "ty", swap)
    kept = doubling_sum(kept, "tx")
    other = lax.ppermute(kept, "ty", swap)
    return jnp.where(side == 0, jnp.concatenate([kept, other]), jnp.concatenate([other, kept]))


def apply_kernel(rows_ref, cols_ref, jac_ref, root_ref, base_ref, out_ref, acc_ref):
    nblk = root_ref.shape[0]
    acc_ref[...] = jnp.zeros(acc_ref.shape, jnp.float32)

    def step(n, carry):
        slot = rows_ref[n]
        acc_ref[slot] = acc_ref[slot] + jnp.dot(
            jac_ref[n], root_ref[cols_ref[n]], preferred_element_type=jnp.float32)
        return carry

    lax.fori_loop(0, jac_ref.shape[0], step, 0)
    base_ref[...] = root_ref[...].astype(jnp.float32) + acc_ref[:nblk]
    out_ref[...] = acc_ref[nblk:]


def apply_blocks(jac_rows, jac_cols, jac_blocks, root_blocks, slot_count):
    nblk, block, width = root_blocks.shape
    smem = pl.BlockSpec(memory_space=pltpu.SMEM)
    vmem = pl.BlockSpec(memory_space=pltpu.VMEM)
    return pl.pallas_call(
        apply_kernel,
        out_shape=(
            jax.ShapeDtypeStruct((nblk, block, width), jnp.float32),
            jax.ShapeDtypeStruct((slot_count - nblk, block, width), jnp.float32),
        ),
        in_specs=[smem, smem, vmem, vmem],
        out_specs=(vmem, vmem),
        scratch_shapes=[pltpu.VMEM((slot_count, block, width), jnp.float32)],
    )(jac_rows, jac_cols, jac_blocks, root_blocks)


def land_kernel(landing_ref, base_ref, *refs):
    pieces = refs[:4]
    forecast_ref, tiles_ref, acc_ref = refs[4:]
    nblk, block, width = base_ref.shape
    rim = pieces[0].shape[0]
    acc_ref[...] = base_ref[...]
    for k in range(4):
        for h in range(rim):
            target = landing_ref[k * rim + h]
            acc_ref[target] = acc_ref[target] + pieces[k][h]
    for i in range(nblk):
        forecast_ref[i * block:(i + 1) * block, :] = acc_ref[i]
    whole = forecast_ref[...]
    gram = lax.dot_general(whole, whole, (((0,), (0,)), ((), ())), precision=HI,
                           preferred_element_type=jnp.float32)
    tiles = width // block
    t = 0
    for a in range(tiles):
        for b in range(a, tiles):
            tiles_ref[t] = gram[a * block:(a + 1) * block, b * block:(b + 1) * block]
            t += 1


def land_and_gram(landing, base, pieces):
    nblk, block, width = base.shape
    tiles = width // block
    count = tiles * (tiles + 1) // 2
    smem = pl.BlockSpec(memory_space=pltpu.SMEM)
    vmem = pl.BlockSpec(memory_space=pltpu.VMEM)
    return pl.pallas_call(
        land_kernel,
        out_shape=(
            jax.ShapeDtypeStruct((nblk * block, width), jnp.float32),
            jax.ShapeDtypeStruct((count, block, block), jnp.float32),
        ),
        in_specs=[smem, vmem] + [vmem] * len(pieces),
        out_specs=(vmem, vmem),
        scratch_shapes=[pltpu.VMEM((nblk, block, width), jnp.float32)],
    )(landing, base, *pieces)

def per_device(jac_blocks, jac_rows, jac_cols, landing, covariance_root):
    nnz, block, _ = jac_blocks.shape
    state_rows, mode_columns = covariance_root.shape
    nblk = state_rows // block
    rim = landing.shape[0] // 4
    slot_count = nblk + 4 * rim
    blocks = covariance_root.reshape(nblk, block, mode_columns)
    base, outgoing = apply_blocks(jac_rows, jac_cols, jac_blocks, blocks, slot_count)
    from_next_x = shifted(outgoing[0:rim], "tx", -1)
    from_prev_x = shifted(outgoing[rim:2 * rim], "tx", 1)
    from_next_y = shifted(outgoing[2 * rim:3 * rim], "ty", -1)
    from_prev_y = shifted(outgoing[3 * rim:], "ty", 1)
    predicted_root, local_tiles = land_and_gram(
        landing, base, [from_next_x, from_prev_x, from_next_y, from_prev_y])
    total_rows = state_rows * lax.axis_size("tx") * lax.axis_size("ty")
    tiles = mode_columns // block
    upper_sum = reduce_tiles(local_tiles)
    position = {}
    counter = 0
    for first in range(tiles):
        for second in range(first, tiles):
            position[first, second] = counter
            counter = counter + 1
    band_rows = []
    for first in range(tiles):
        pieces = []
        for second in range(tiles):
            if first <= second:
                pieces.append(upper_sum[position[first, second]])
            else:
                pieces.append(upper_sum[position[second, first]].T)
        band_rows.append(jnp.concatenate(pieces, axis=1))
    summed = jnp.concatenate(band_rows, axis=0)
    inner_products_table = summed / total_rows
    rescaled_orthogonal_root, r_factor = factor_solve(inner_products_table, predicted_root, block)
    return (rescaled_orthogonal_root, r_factor)


def solution(mesh):
    placed = (
        P(("basin", "tx", "ty"), None, None),
        P(("basin", "tx", "ty")),
        P(("basin", "tx", "ty")),
        P(("basin", "tx", "ty")),
        P(("basin", "tx", "ty"), None),
    )
    return jax.shard_map(
        per_device,
        mesh=mesh,
        in_specs=placed,
        out_specs=(P(("basin", "tx", "ty"), None), P("basin", None)),
        check_vma=False,
    )
```

```python
import jax
import jax.numpy as jnp
from jax import lax
from jax.experimental import pallas as pl
from jax.experimental.pallas import tpu as pltpu
from jax.sharding import PartitionSpec as P

HI = lax.Precision.HIGHEST


def factor_kernel(g_ref, f_ref, x_ref, u_ref, w_ref, inv_ref, xs_ref):
    n = g_ref.shape[0]
    b = inv_ref.shape[1]
    nb = n // b
    w_ref[...] = g_ref[...]
    u_ref[...] = jnp.zeros(u_ref.shape, jnp.float32)
    lane = lax.broadcasted_iota(jnp.int32, (1, b), 1)
    rows = lax.broadcasted_iota(jnp.int32, (b, 1), 0)
    eye = jnp.where(lax.broadcasted_iota(jnp.int32, (b, b), 0) == lax.broadcasted_iota(jnp.int32, (b, b), 1), 1.0, 0.0)
    for k in range(nb):
        o = k * b
        inv_ref[k] = eye
        for j in range(b):
            r = w_ref[o + j:o + j + 1, o:o + b]
            rs = lax.rsqrt(r[:, j:j + 1])
            u = jnp.where(lane >= j, r, 0.0) * rs
            u_ref[o + j:o + j + 1, o:o + b] = u
            brow = inv_ref[k, j:j + 1, :] * rs
            inv_ref[k, j:j + 1, :] = brow
            if j == b - 1:
                break
            s = (j + 1) // 8 * 8
            v = w_ref[o + s:o + b, o + j:o + j + 1] * rs
            v = jnp.where(rows[s:] > j, v, 0.0)
            w_ref[o + s:o + b, o:o + b] = w_ref[o + s:o + b, o:o + b] - v * u
            inv_ref[k, s:, :] = inv_ref[k, s:, :] - v * brow
        if k < nb - 1:
            e = o + b
            panel = jnp.dot(inv_ref[k], w_ref[o:e, e:], precision=HI, preferred_element_type=jnp.float32)
            u_ref[o:e, e:] = panel
            w_ref[e:, e:] = w_ref[e:, e:] - lax.dot_general(
                panel, panel, (((0,), (0,)), ((), ())), precision=HI, preferred_element_type=jnp.float32)
    for k in range(nb):
        o = k * b
        y = f_ref[:, o:o + b]
        if k > 0:
            y = y - jnp.dot(xs_ref[:, :o], u_ref[:o, o:o + b], precision=HI, preferred_element_type=jnp.float32)
        xs_ref[:, o:o + b] = lax.dot_general(
            y, inv_ref[k], (((1,), (1,)), ((), ())), precision=HI, preferred_element_type=jnp.float32)
    x_ref[...] = xs_ref[...].astype(x_ref.dtype)


def factor_solve(gram, forecast, block=128):
    n = gram.shape[0]
    m = forecast.shape[0]
    vmem = pl.BlockSpec(memory_space=pltpu.VMEM)
    return pl.pallas_call(
        factor_kernel,
        out_shape=(jax.ShapeDtypeStruct((m, n), jnp.bfloat16), jax.ShapeDtypeStruct((n, n), jnp.float32)),
        in_specs=[vmem, vmem],
        out_specs=(vmem, vmem),
        scratch_shapes=[
            pltpu.VMEM((n, n), jnp.float32),
            pltpu.VMEM((n // block, block, block), jnp.float32),
            pltpu.VMEM((m, n), jnp.float32),
        ],
    )(gram, forecast)


def shifted(block, axis, distance):
    devices = range(lax.axis_size(axis))
    route = [(i - distance, i) for i in devices if i - distance in devices]
    return lax.ppermute(block, axis, route)


def doubling_sum(block, axis):
    size = lax.axis_size(axis)
    distance = 1
    while distance < size:
        route = [(i, i ^ distance) for i in range(size)]
        block = block + lax.ppermute(block, axis, route)
        distance *= 2
    return block


def reduce_tiles(tiles):
    count = tiles.shape[0]
    if lax.axis_size("ty") != 2 or count % 2:
        return doubling_sum(doubling_sum(tiles, "tx"), "ty")
    half = count // 2
    side = lax.axis_index("ty")
    swap = [(0, 1), (1, 0)]
    sent = lax.dynamic_slice_in_dim(tiles, (1 - side) * half, half, axis=0)
    kept = lax.dynamic_slice_in_dim(tiles, side * half, half, axis=0)
    kept = kept + lax.ppermute(sent, "ty", swap)
    kept = doubling_sum(kept, "tx")
    other = lax.ppermute(kept, "ty", swap)
    return jnp.where(side == 0, jnp.concatenate([kept, other]), jnp.concatenate([other, kept]))


def halving_sum(flat):
    levels = []
    for axis in ("ty", "tx"):
        size = lax.axis_size(axis)
        distance = 1
        while distance < size:
            levels.append((axis, size, distance))
            distance *= 2
    pieces = 2 ** len(levels)
    regular = all(size & (size - 1) == 0 for _, size, _ in levels)
    if not regular or flat.shape[0] % pieces:
        return doubling_sum(doubling_sum(flat, "tx"), "ty")
    bits = []
    for axis, size, distance in levels:
        bit = lax.axis_index(axis) // distance % 2
        route = [(i, i ^ distance) for i in range(size)]
        half = flat.shape[0] // 2
        sent = lax.dynamic_slice_in_dim(flat, (1 - bit) * half, half)
        kept = lax.dynamic_slice_in_dim(flat, bit * half, half)
        flat = kept + lax.ppermute(sent, axis, route)
        bits.append(bit)
    for (axis, size, distance), bit in reversed(list(zip(levels, bits))):
        route = [(i, i ^ distance) for i in range(size)]
        other = lax.ppermute(flat, axis, route)
        flat = jnp.where(bit == 0, jnp.concatenate([flat, other]), jnp.concatenate([other, flat]))
    return flat


def apply_kernel(rows_ref, cols_ref, jac_ref, root_ref, base_ref, *refs):
    out_refs = refs[:-1]
    acc_ref = refs[-1]
    nblk = root_ref.shape[0]
    rim = out_refs[0].shape[0]
    acc_ref[...] = jnp.zeros(acc_ref.shape, jnp.float32)

    def step(n, carry):
        slot = rows_ref[n]
        acc_ref[slot] = acc_ref[slot] + jnp.dot(
            jac_ref[n], root_ref[cols_ref[n]], preferred_element_type=jnp.float32)
        return carry

    lax.fori_loop(0, jac_ref.shape[0], step, 0)
    base_ref[...] = root_ref[...].astype(jnp.float32) + acc_ref[:nblk]
    for k, out_ref in enumerate(out_refs):
        out_ref[...] = acc_ref[nblk + k * rim:nblk + (k + 1) * rim]


def apply_blocks(jac_rows, jac_cols, jac_blocks, root_blocks, slot_count):
    nblk, block, width = root_blocks.shape
    rim = (slot_count - nblk) // 4
    smem = pl.BlockSpec(memory_space=pltpu.SMEM)
    vmem = pl.BlockSpec(memory_space=pltpu.VMEM)
    return pl.pallas_call(
        apply_kernel,
        out_shape=(jax.ShapeDtypeStruct((nblk, block, width), jnp.float32),)
        + tuple(jax.ShapeDtypeStruct((rim, block, width), jnp.float32) for _ in range(4)),
        in_specs=[smem, smem, vmem, vmem],
        out_specs=(vmem,) * 5,
        scratch_shapes=[pltpu.VMEM((slot_count, block, width), jnp.float32)],
    )(jac_rows, jac_cols, jac_blocks, root_blocks)


def land_kernel(landing_ref, base_ref, *refs):
    pieces = refs[:4]
    forecast_ref, tiles_ref, acc_ref = refs[4:]
    nblk, block, width = base_ref.shape
    rim = pieces[0].shape[0]
    acc_ref[...] = base_ref[...]
    for k in range(4):
        for h in range(rim):
            target = landing_ref[k * rim + h]
            acc_ref[target] = acc_ref[target] + pieces[k][h]
    for i in range(nblk):
        forecast_ref[i * block:(i + 1) * block, :] = acc_ref[i]
    whole = forecast_ref[...]
    gram = lax.dot_general(whole, whole, (((0,), (0,)), ((), ())), precision=HI,
                           preferred_element_type=jnp.float32)
    tiles = width // block
    t = 0
    for a in range(tiles):
        for b in range(a, tiles):
            tiles_ref[t] = gram[a * block:(a + 1) * block, b * block:(b + 1) * block]
            t += 1


def land_and_gram(landing, base, pieces):
    nblk, block, width = base.shape
    tiles = width // block
    count = tiles * (tiles + 1) // 2
    smem = pl.BlockSpec(memory_space=pltpu.SMEM)
    vmem = pl.BlockSpec(memory_space=pltpu.VMEM)
    return pl.pallas_call(
        land_kernel,
        out_shape=(
            jax.ShapeDtypeStruct((nblk * block, width), jnp.float32),
            jax.ShapeDtypeStruct((count, block, block), jnp.float32),
        ),
        in_specs=[smem, vmem] + [vmem] * len(pieces),
        out_specs=(vmem, vmem),
        scratch_shapes=[pltpu.VMEM((nblk, block, width), jnp.float32)],
    )(landing, base, *pieces)

def per_device(jac_blocks, jac_rows, jac_cols, landing, covariance_root):
    nnz, block, _ = jac_blocks.shape
    state_rows, mode_columns = covariance_root.shape
    nblk = state_rows // block
    rim = landing.shape[0] // 4
    slot_count = nblk + 4 * rim
    blocks = covariance_root.reshape(nblk, block, mode_columns)
    base, to_prev_x, to_next_x, to_prev_y, to_next_y = apply_blocks(
        jac_rows, jac_cols, jac_blocks, blocks, slot_count)
    from_next_x = shifted(to_prev_x, "tx", -1)
    from_prev_x = shifted(to_next_x, "tx", 1)
    from_next_y = shifted(to_prev_y, "ty", -1)
    from_prev_y = shifted(to_next_y, "ty", 1)
    predicted_root, local_tiles = land_and_gram(
        landing, base, [from_next_x, from_prev_x, from_next_y, from_prev_y])
    total_rows = state_rows * lax.axis_size("tx") * lax.axis_size("ty")
    tiles = mode_columns // block
    upper_sum = halving_sum(local_tiles.reshape(-1)).reshape(local_tiles.shape)
    position = {}
    counter = 0
    for first in range(tiles):
        for second in range(first, tiles):
            position[first, second] = counter
            counter = counter + 1
    band_rows = []
    for first in range(tiles):
        pieces = []
        for second in range(tiles):
            if first <= second:
                pieces.append(upper_sum[position[first, second]])
            else:
                pieces.append(upper_sum[position[second, first]].T)
        band_rows.append(jnp.concatenate(pieces, axis=1))
    summed = jnp.concatenate(band_rows, axis=0)
    inner_products_table = summed / total_rows
    rescaled_orthogonal_root, r_factor = factor_solve(inner_products_table, predicted_root, block)
    return (rescaled_orthogonal_root, r_factor)


def solution(mesh):
    placed = (
        P(("basin", "tx", "ty"), None, None),
        P(("basin", "tx", "ty")),
        P(("basin", "tx", "ty")),
        P(("basin", "tx", "ty")),
        P(("basin", "tx", "ty"), None),
    )
    return jax.shard_map(
        per_device,
        mesh=mesh,
        in_specs=placed,
        out_specs=(P(("basin", "tx", "ty"), None), P("basin", None)),
        check_vma=False,
    )
```

```python
import jax
import jax.numpy as jnp
from jax import lax
from jax.experimental import pallas as pl
from jax.experimental.pallas import tpu as pltpu
from jax.sharding import PartitionSpec as P

HI = lax.Precision.HIGHEST


def factor_kernel(g_ref, f_ref, x_ref, u_ref, w_ref, inv_ref, xs_ref):
    n = g_ref.shape[0]
    b = inv_ref.shape[1]
    nb = n // b
    w_ref[...] = g_ref[...]
    u_ref[...] = jnp.zeros(u_ref.shape, jnp.float32)
    lane = lax.broadcasted_iota(jnp.int32, (1, b), 1)
    rows = lax.broadcasted_iota(jnp.int32, (b, 1), 0)
    eye = jnp.where(lax.broadcasted_iota(jnp.int32, (b, b), 0) == lax.broadcasted_iota(jnp.int32, (b, b), 1), 1.0, 0.0)
    for k in range(nb):
        o = k * b
        inv_ref[k] = eye
        for j in range(b):
            r = w_ref[o + j:o + j + 1, o:o + b]
            rs = lax.rsqrt(r[:, j:j + 1])
            u = jnp.where(lane >= j, r, 0.0) * rs
            u_ref[o + j:o + j + 1, o:o + b] = u
            brow = inv_ref[k, j:j + 1, :] * rs
            inv_ref[k, j:j + 1, :] = brow
            if j == b - 1:
                break
            s = (j + 1) // 8 * 8
            v = w_ref[o + s:o + b, o + j:o + j + 1] * rs
            v = jnp.where(rows[s:] > j, v, 0.0)
            w_ref[o + s:o + b, o:o + b] = w_ref[o + s:o + b, o:o + b] - v * u
            inv_ref[k, s:, :] = inv_ref[k, s:, :] - v * brow
        if k < nb - 1:
            e = o + b
            panel = jnp.dot(inv_ref[k], w_ref[o:e, e:], precision=HI, preferred_element_type=jnp.float32)
            u_ref[o:e, e:] = panel
            w_ref[e:, e:] = w_ref[e:, e:] - lax.dot_general(
                panel, panel, (((0,), (0,)), ((), ())), precision=HI, preferred_element_type=jnp.float32)
    for k in range(nb):
        o = k * b
        y = f_ref[:, o:o + b]
        if k > 0:
            y = y - jnp.dot(xs_ref[:, :o], u_ref[:o, o:o + b], precision=HI, preferred_element_type=jnp.float32)
        xs_ref[:, o:o + b] = lax.dot_general(
            y, inv_ref[k], (((1,), (1,)), ((), ())), precision=HI, preferred_element_type=jnp.float32)
    x_ref[...] = xs_ref[...].astype(x_ref.dtype)


def factor_solve(gram, forecast, block=128):
    n = gram.shape[0]
    m = forecast.shape[0]
    vmem = pl.BlockSpec(memory_space=pltpu.VMEM)
    return pl.pallas_call(
        factor_kernel,
        out_shape=(jax.ShapeDtypeStruct((m, n), jnp.bfloat16), jax.ShapeDtypeStruct((n, n), jnp.float32)),
        in_specs=[vmem, vmem],
        out_specs=(vmem, vmem),
        scratch_shapes=[
            pltpu.VMEM((n, n), jnp.float32),
            pltpu.VMEM((n // block, block, block), jnp.float32),
            pltpu.VMEM((m, n), jnp.float32),
        ],
    )(gram, forecast)


def shifted(block, axis, distance):
    devices = range(lax.axis_size(axis))
    route = [(i - distance, i) for i in devices if i - distance in devices]
    return lax.ppermute(block, axis, route)


def doubling_sum(block, axis):
    size = lax.axis_size(axis)
    distance = 1
    while distance < size:
        route = [(i, i ^ distance) for i in range(size)]
        block = block + lax.ppermute(block, axis, route)
        distance *= 2
    return block


def reduce_tiles(tiles):
    count = tiles.shape[0]
    if lax.axis_size("ty") != 2 or count % 2:
        return doubling_sum(doubling_sum(tiles, "tx"), "ty")
    half = count // 2
    side = lax.axis_index("ty")
    swap = [(0, 1), (1, 0)]
    sent = lax.dynamic_slice_in_dim(tiles, (1 - side) * half, half, axis=0)
    kept = lax.dynamic_slice_in_dim(tiles, side * half, half, axis=0)
    kept = kept + lax.ppermute(sent, "ty", swap)
    kept = doubling_sum(kept, "tx")
    other = lax.ppermute(kept, "ty", swap)
    return jnp.where(side == 0, jnp.concatenate([kept, other]), jnp.concatenate([other, kept]))


def group_levels():
    levels = []
    for axis, width in (("ty", 1), ("tx", 2)):
        size = lax.axis_size(axis)
        if size & (size - 1):
            return None
        stride = 1
        while stride < size:
            bits = min(width, (size // stride).bit_length() - 1)
            levels.append((axis, size, stride, 2 ** bits))
            stride *= 2 ** bits
    return levels


def grouped_sum(flat):
    levels = group_levels()
    if levels is None:
        return doubling_sum(doubling_sum(flat, "tx"), "ty")
    pieces = 1
    for level in levels:
        pieces *= level[3]
    if flat.shape[0] % pieces:
        return doubling_sum(doubling_sum(flat, "tx"), "ty")
    digits = []
    for axis, size, stride, group in levels:
        digit = lax.axis_index(axis) // stride % group
        chunk = flat.shape[0] // group
        kept = lax.dynamic_slice_in_dim(flat, digit * chunk, chunk)
        for offset in range(1, group):
            route = [(i, i ^ (offset * stride)) for i in range(size)]
            sent = lax.dynamic_slice_in_dim(flat, (digit ^ offset) * chunk, chunk)
            kept = kept + lax.ppermute(sent, axis, route)
        flat = kept
        digits.append(digit)
    for (axis, size, stride, group), digit in reversed(list(zip(levels, digits))):
        got = [flat]
        for offset in range(1, group):
            route = [(i, i ^ (offset * stride)) for i in range(size)]
            got.append(lax.ppermute(flat, axis, route))
        placed = []
        for position in range(group):
            pick = got[0]
            for offset in range(1, group):
                pick = jnp.where((digit ^ offset) == position, got[offset], pick)
            placed.append(pick)
        flat = jnp.concatenate(placed)
    return flat


def apply_kernel(rows_ref, cols_ref, jac_ref, root_ref, base_ref, *refs):
    out_refs = refs[:-1]
    acc_ref = refs[-1]
    nblk = root_ref.shape[0]
    rim = out_refs[0].shape[0]
    acc_ref[...] = jnp.zeros(acc_ref.shape, jnp.float32)

    def step(n, carry):
        slot = rows_ref[n]
        acc_ref[slot] = acc_ref[slot] + jnp.dot(
            jac_ref[n], root_ref[cols_ref[n]], preferred_element_type=jnp.float32)
        return carry

    lax.fori_loop(0, jac_ref.shape[0], step, 0, unroll=True)
    base_ref[...] = root_ref[...].astype(jnp.float32) + acc_ref[:nblk]
    for k, out_ref in enumerate(out_refs):
        out_ref[...] = acc_ref[nblk + k * rim:nblk + (k + 1) * rim]


def apply_blocks(jac_rows, jac_cols, jac_blocks, root_blocks, slot_count):
    nblk, block, width = root_blocks.shape
    rim = (slot_count - nblk) // 4
    smem = pl.BlockSpec(memory_space=pltpu.SMEM)
    vmem = pl.BlockSpec(memory_space=pltpu.VMEM)
    return pl.pallas_call(
        apply_kernel,
        out_shape=(jax.ShapeDtypeStruct((nblk, block, width), jnp.float32),)
        + tuple(jax.ShapeDtypeStruct((rim, block, width), jnp.float32) for _ in range(4)),
        in_specs=[smem, smem, vmem, vmem],
        out_specs=(vmem,) * 5,
        scratch_shapes=[pltpu.VMEM((slot_count, block, width), jnp.float32)],
    )(jac_rows, jac_cols, jac_blocks, root_blocks)


def land_kernel(landing_ref, base_ref, *refs):
    pieces = refs[:4]
    forecast_ref, tiles_ref, acc_ref = refs[4:]
    nblk, block, width = base_ref.shape
    rim = pieces[0].shape[0]
    acc_ref[...] = base_ref[...]
    for k in range(4):
        for h in range(rim):
            target = landing_ref[k * rim + h]
            acc_ref[target] = acc_ref[target] + pieces[k][h]
    for i in range(nblk):
        forecast_ref[i * block:(i + 1) * block, :] = acc_ref[i]
    whole = forecast_ref[...]
    gram = lax.dot_general(whole, whole, (((0,), (0,)), ((), ())), precision=HI,
                           preferred_element_type=jnp.float32)
    tiles = width // block
    t = 0
    for a in range(tiles):
        for b in range(a, tiles):
            tiles_ref[t] = gram[a * block:(a + 1) * block, b * block:(b + 1) * block]
            t += 1


def land_and_gram(landing, base, pieces):
    nblk, block, width = base.shape
    tiles = width // block
    count = tiles * (tiles + 1) // 2
    smem = pl.BlockSpec(memory_space=pltpu.SMEM)
    vmem = pl.BlockSpec(memory_space=pltpu.VMEM)
    return pl.pallas_call(
        land_kernel,
        out_shape=(
            jax.ShapeDtypeStruct((nblk * block, width), jnp.float32),
            jax.ShapeDtypeStruct((count, block, block), jnp.float32),
        ),
        in_specs=[smem, vmem] + [vmem] * len(pieces),
        out_specs=(vmem, vmem),
        scratch_shapes=[pltpu.VMEM((nblk, block, width), jnp.float32)],
    )(landing, base, *pieces)

def per_device(jac_blocks, jac_rows, jac_cols, landing, covariance_root):
    nnz, block, _ = jac_blocks.shape
    state_rows, mode_columns = covariance_root.shape
    nblk = state_rows // block
    rim = landing.shape[0] // 4
    slot_count = nblk + 4 * rim
    blocks = covariance_root.reshape(nblk, block, mode_columns)
    base, to_prev_x, to_next_x, to_prev_y, to_next_y = apply_blocks(
        jac_rows, jac_cols, jac_blocks, blocks, slot_count)
    from_next_x = shifted(to_prev_x, "tx", -1)
    from_prev_x = shifted(to_next_x, "tx", 1)
    from_next_y = shifted(to_prev_y, "ty", -1)
    from_prev_y = shifted(to_next_y, "ty", 1)
    predicted_root, local_tiles = land_and_gram(
        landing, base, [from_next_x, from_prev_x, from_next_y, from_prev_y])
    total_rows = state_rows * lax.axis_size("tx") * lax.axis_size("ty")
    tiles = mode_columns // block
    upper_sum = grouped_sum(local_tiles.reshape(-1)).reshape(local_tiles.shape)
    position = {}
    counter = 0
    for first in range(tiles):
        for second in range(first, tiles):
            position[first, second] = counter
            counter = counter + 1
    band_rows = []
    for first in range(tiles):
        pieces = []
        for second in range(tiles):
            if first <= second:
                pieces.append(upper_sum[position[first, second]])
            else:
                pieces.append(upper_sum[position[second, first]].T)
        band_rows.append(jnp.concatenate(pieces, axis=1))
    summed = jnp.concatenate(band_rows, axis=0)
    inner_products_table = summed / total_rows
    rescaled_orthogonal_root, r_factor = factor_solve(inner_products_table, predicted_root, block)
    return (rescaled_orthogonal_root, r_factor)


def solution(mesh):
    placed = (
        P(("basin", "tx", "ty"), None, None),
        P(("basin", "tx", "ty")),
        P(("basin", "tx", "ty")),
        P(("basin", "tx", "ty")),
        P(("basin", "tx", "ty"), None),
    )
    return jax.shard_map(
        per_device,
        mesh=mesh,
        in_specs=placed,
        out_specs=(P(("basin", "tx", "ty"), None), P("basin", None)),
        check_vma=False,
    )
```

```python
import functools

import jax
import jax.numpy as jnp
from jax import lax
from jax.experimental import pallas as pl
from jax.experimental.pallas import tpu as pltpu
from jax.sharding import PartitionSpec as P

HI = lax.Precision.HIGHEST


def factor_kernel(total, g_ref, f_ref, x_ref, u_ref, w_ref, inv_ref, xs_ref):
    n = f_ref.shape[1]
    b = inv_ref.shape[1]
    nb = n // b
    t = 0
    for first in range(nb):
        for second in range(first, nb):
            tile = g_ref[t] / total
            w_ref[first * b:(first + 1) * b, second * b:(second + 1) * b] = tile
            if second > first:
                w_ref[second * b:(second + 1) * b, first * b:(first + 1) * b] = tile.T
            t += 1
    u_ref[...] = jnp.zeros(u_ref.shape, jnp.float32)
    lane = lax.broadcasted_iota(jnp.int32, (1, b), 1)
    rows = lax.broadcasted_iota(jnp.int32, (b, 1), 0)
    eye = jnp.where(lax.broadcasted_iota(jnp.int32, (b, b), 0) == lax.broadcasted_iota(jnp.int32, (b, b), 1), 1.0, 0.0)
    for k in range(nb):
        o = k * b
        inv_ref[k] = eye
        for j in range(b):
            r = w_ref[o + j:o + j + 1, o:o + b]
            rs = lax.rsqrt(r[:, j:j + 1])
            u = jnp.where(lane >= j, r, 0.0) * rs
            u_ref[o + j:o + j + 1, o:o + b] = u
            brow = inv_ref[k, j:j + 1, :] * rs
            inv_ref[k, j:j + 1, :] = brow
            if j == b - 1:
                break
            s = (j + 1) // 8 * 8
            v = w_ref[o + s:o + b, o + j:o + j + 1] * rs
            v = jnp.where(rows[s:] > j, v, 0.0)
            w_ref[o + s:o + b, o:o + b] = w_ref[o + s:o + b, o:o + b] - v * u
            inv_ref[k, s:, :] = inv_ref[k, s:, :] - v * brow
        if k < nb - 1:
            e = o + b
            panel = jnp.dot(inv_ref[k], w_ref[o:e, e:], precision=HI, preferred_element_type=jnp.float32)
            u_ref[o:e, e:] = panel
            w_ref[e:, e:] = w_ref[e:, e:] - lax.dot_general(
                panel, panel, (((0,), (0,)), ((), ())), precision=HI, preferred_element_type=jnp.float32)
    for k in range(nb):
        o = k * b
        y = f_ref[:, o:o + b]
        if k > 0:
            y = y - jnp.dot(xs_ref[:, :o], u_ref[:o, o:o + b], precision=HI, preferred_element_type=jnp.float32)
        xs_ref[:, o:o + b] = lax.dot_general(
            y, inv_ref[k], (((1,), (1,)), ((), ())), precision=HI, preferred_element_type=jnp.float32)
    x_ref[...] = xs_ref[...].astype(x_ref.dtype)


def factor_solve(tiles, forecast, total, block=128):
    n = forecast.shape[1]
    m = forecast.shape[0]
    vmem = pl.BlockSpec(memory_space=pltpu.VMEM)
    return pl.pallas_call(
        functools.partial(factor_kernel, float(total)),
        out_shape=(jax.ShapeDtypeStruct((m, n), jnp.bfloat16), jax.ShapeDtypeStruct((n, n), jnp.float32)),
        in_specs=[vmem, vmem],
        out_specs=(vmem, vmem),
        scratch_shapes=[
            pltpu.VMEM((n, n), jnp.float32),
            pltpu.VMEM((n // block, block, block), jnp.float32),
            pltpu.VMEM((m, n), jnp.float32),
        ],
    )(tiles, forecast)


def shifted(block, axis, distance):
    devices = range(lax.axis_size(axis))
    route = [(i - distance, i) for i in devices if i - distance in devices]
    return lax.ppermute(block, axis, route)


def doubling_sum(block, axis):
    size = lax.axis_size(axis)
    distance = 1
    while distance < size:
        route = [(i, i ^ distance) for i in range(size)]
        block = block + lax.ppermute(block, axis, route)
        distance *= 2
    return block


def reduce_tiles(tiles):
    count = tiles.shape[0]
    if lax.axis_size("ty") != 2 or count % 2:
        return doubling_sum(doubling_sum(tiles, "tx"), "ty")
    half = count // 2
    side = lax.axis_index("ty")
    swap = [(0, 1), (1, 0)]
    sent = lax.dynamic_slice_in_dim(tiles, (1 - side) * half, half, axis=0)
    kept = lax.dynamic_slice_in_dim(tiles, side * half, half, axis=0)
    kept = kept + lax.ppermute(sent, "ty", swap)
    kept = doubling_sum(kept, "tx")
    other = lax.ppermute(kept, "ty", swap)
    return jnp.where(side == 0, jnp.concatenate([kept, other]), jnp.concatenate([other, kept]))


def group_levels():
    levels = []
    for axis, width in (("ty", 1), ("tx", 2)):
        size = lax.axis_size(axis)
        if size & (size - 1):
            return None
        stride = 1
        while stride < size:
            bits = min(width, (size // stride).bit_length() - 1)
            levels.append((axis, size, stride, 2 ** bits))
            stride *= 2 ** bits
    return levels


def grouped_sum(flat):
    levels = group_levels()
    if levels is None:
        return doubling_sum(doubling_sum(flat, "tx"), "ty")
    pieces = 1
    for level in levels:
        pieces *= level[3]
    if flat.shape[0] % pieces:
        return doubling_sum(doubling_sum(flat, "tx"), "ty")
    digits = []
    for axis, size, stride, group in levels:
        digit = lax.axis_index(axis) // stride % group
        chunk = flat.shape[0] // group
        kept = lax.dynamic_slice_in_dim(flat, digit * chunk, chunk)
        for offset in range(1, group):
            route = [(i, i ^ (offset * stride)) for i in range(size)]
            sent = lax.dynamic_slice_in_dim(flat, (digit ^ offset) * chunk, chunk)
            kept = kept + lax.ppermute(sent, axis, route)
        flat = kept
        digits.append(digit)
    for (axis, size, stride, group), digit in reversed(list(zip(levels, digits))):
        got = [flat]
        for offset in range(1, group):
            route = [(i, i ^ (offset * stride)) for i in range(size)]
            got.append(lax.ppermute(flat, axis, route))
        placed = []
        for position in range(group):
            pick = got[0]
            for offset in range(1, group):
                pick = jnp.where((digit ^ offset) == position, got[offset], pick)
            placed.append(pick)
        flat = jnp.concatenate(placed)
    return flat


def apply_kernel(own, rows_ref, cols_ref, jac_ref, root_ref, *refs):
    out_refs = refs[:-1]
    acc_ref = refs[-1]
    nblk = root_ref.shape[0]
    first = 0 if own else nblk
    acc_ref[...] = jnp.zeros(acc_ref.shape, jnp.float32)

    def step(n, carry):
        slot = rows_ref[n]
        inside = slot < nblk if own else slot >= nblk

        @pl.when(inside)
        def _():
            acc_ref[slot - first] = acc_ref[slot - first] + jnp.dot(
                jac_ref[n], root_ref[cols_ref[n]], preferred_element_type=jnp.float32)

        return carry

    lax.fori_loop(0, jac_ref.shape[0], step, 0, unroll=True)
    if own:
        out_refs[0][...] = root_ref[...].astype(jnp.float32) + acc_ref[...]
    else:
        rim = out_refs[0].shape[0]
        for k, out_ref in enumerate(out_refs):
            out_ref[...] = acc_ref[k * rim:(k + 1) * rim]


def apply_blocks(jac_rows, jac_cols, jac_blocks, root_blocks, slot_count, own):
    nblk, block, width = root_blocks.shape
    rim = (slot_count - nblk) // 4
    smem = pl.BlockSpec(memory_space=pltpu.SMEM)
    vmem = pl.BlockSpec(memory_space=pltpu.VMEM)
    if own:
        shapes = (jax.ShapeDtypeStruct((nblk, block, width), jnp.float32),)
        held = nblk
    else:
        shapes = tuple(jax.ShapeDtypeStruct((rim, block, width), jnp.float32) for _ in range(4))
        held = 4 * rim
    return pl.pallas_call(
        functools.partial(apply_kernel, own),
        out_shape=shapes,
        in_specs=[smem, smem, vmem, vmem],
        out_specs=(vmem,) * len(shapes),
        scratch_shapes=[pltpu.VMEM((held, block, width), jnp.float32)],
    )(jac_rows, jac_cols, jac_blocks, root_blocks)


def land_kernel(landing_ref, base_ref, *refs):
    pieces = refs[:4]
    forecast_ref, tiles_ref, acc_ref = refs[4:]
    nblk, block, width = base_ref.shape
    rim = pieces[0].shape[0]
    acc_ref[...] = base_ref[...]
    for k in range(4):
        for h in range(rim):
            target = landing_ref[k * rim + h]
            acc_ref[target] = acc_ref[target] + pieces[k][h]
    for i in range(nblk):
        forecast_ref[i * block:(i + 1) * block, :] = acc_ref[i]
    whole = forecast_ref[...]
    gram = lax.dot_general(whole, whole, (((0,), (0,)), ((), ())), precision=HI,
                           preferred_element_type=jnp.float32)
    tiles = width // block
    t = 0
    for a in range(tiles):
        for b in range(a, tiles):
            tiles_ref[t] = gram[a * block:(a + 1) * block, b * block:(b + 1) * block]
            t += 1


def land_and_gram(landing, base, pieces):
    nblk, block, width = base.shape
    tiles = width // block
    count = tiles * (tiles + 1) // 2
    smem = pl.BlockSpec(memory_space=pltpu.SMEM)
    vmem = pl.BlockSpec(memory_space=pltpu.VMEM)
    return pl.pallas_call(
        land_kernel,
        out_shape=(
            jax.ShapeDtypeStruct((nblk * block, width), jnp.float32),
            jax.ShapeDtypeStruct((count, block, block), jnp.float32),
        ),
        in_specs=[smem, vmem] + [vmem] * len(pieces),
        out_specs=(vmem, vmem),
        scratch_shapes=[pltpu.VMEM((nblk, block, width), jnp.float32)],
    )(landing, base, *pieces)

def per_device(jac_blocks, jac_rows, jac_cols, landing, covariance_root):
    nnz, block, _ = jac_blocks.shape
    state_rows, mode_columns = covariance_root.shape
    nblk = state_rows // block
    rim = landing.shape[0] // 4
    slot_count = nblk + 4 * rim
    blocks = covariance_root.reshape(nblk, block, mode_columns)
    to_prev_x, to_next_x, to_prev_y, to_next_y = apply_blocks(
        jac_rows, jac_cols, jac_blocks, blocks, slot_count, False)
    from_next_x = shifted(to_prev_x, "tx", -1)
    from_prev_x = shifted(to_next_x, "tx", 1)
    from_next_y = shifted(to_prev_y, "ty", -1)
    from_prev_y = shifted(to_next_y, "ty", 1)
    (base,) = apply_blocks(jac_rows, jac_cols, jac_blocks, blocks, slot_count, True)
    predicted_root, local_tiles = land_and_gram(
        landing, base, [from_next_x, from_prev_x, from_next_y, from_prev_y])
    total_rows = state_rows * lax.axis_size("tx") * lax.axis_size("ty")
    tiles = mode_columns // block
    upper_sum = grouped_sum(local_tiles.reshape(-1)).reshape(local_tiles.shape)
    rescaled_orthogonal_root, r_factor = factor_solve(upper_sum, predicted_root, total_rows, block)
    return (rescaled_orthogonal_root, r_factor)


def solution(mesh):
    placed = (
        P(("basin", "tx", "ty"), None, None),
        P(("basin", "tx", "ty")),
        P(("basin", "tx", "ty")),
        P(("basin", "tx", "ty")),
        P(("basin", "tx", "ty"), None),
    )
    return jax.shard_map(
        per_device,
        mesh=mesh,
        in_specs=placed,
        out_specs=(P(("basin", "tx", "ty"), None), P("basin", None)),
        check_vma=False,
    )
```

```python
import functools

import jax
import jax.numpy as jnp
from jax import lax
from jax.experimental import pallas as pl
from jax.experimental.pallas import tpu as pltpu
from jax.sharding import PartitionSpec as P

HI = lax.Precision.HIGHEST


def factor_kernel(total, g_ref, f_ref, x_ref, u_ref, w_ref, inv_ref, xs_ref):
    n = f_ref.shape[1]
    b = inv_ref.shape[1]
    nb = n // b
    t = 0
    for first in range(nb):
        for second in range(first, nb):
            tile = g_ref[t] / total
            w_ref[first * b:(first + 1) * b, second * b:(second + 1) * b] = tile
            if second > first:
                w_ref[second * b:(second + 1) * b, first * b:(first + 1) * b] = tile.T
            t += 1
    u_ref[...] = jnp.zeros(u_ref.shape, jnp.float32)
    lane = lax.broadcasted_iota(jnp.int32, (1, b), 1)
    rows = lax.broadcasted_iota(jnp.int32, (b, 1), 0)
    eye = jnp.where(lax.broadcasted_iota(jnp.int32, (b, b), 0) == lax.broadcasted_iota(jnp.int32, (b, b), 1), 1.0, 0.0)
    for k in range(nb):
        o = k * b
        inv_ref[k] = eye
        for j in range(b):
            r = w_ref[o + j:o + j + 1, o:o + b]
            rs = lax.rsqrt(r[:, j:j + 1])
            u = jnp.where(lane >= j, r, 0.0) * rs
            u_ref[o + j:o + j + 1, o:o + b] = u
            brow = inv_ref[k, j:j + 1, :] * rs
            inv_ref[k, j:j + 1, :] = brow
            if j == b - 1:
                break
            s = (j + 1) // 8 * 8
            v = w_ref[o + s:o + b, o + j:o + j + 1] * rs
            v = jnp.where(rows[s:] > j, v, 0.0)
            w_ref[o + s:o + b, o:o + b] = w_ref[o + s:o + b, o:o + b] - v * u
            inv_ref[k, s:, :] = inv_ref[k, s:, :] - v * brow
        if k < nb - 1:
            e = o + b
            panel = jnp.dot(inv_ref[k], w_ref[o:e, e:], precision=HI, preferred_element_type=jnp.float32)
            u_ref[o:e, e:] = panel
            w_ref[e:, e:] = w_ref[e:, e:] - lax.dot_general(
                panel, panel, (((0,), (0,)), ((), ())), precision=HI, preferred_element_type=jnp.float32)
    for k in range(nb):
        o = k * b
        y = f_ref[:, o:o + b]
        if k > 0:
            y = y - jnp.dot(xs_ref[:, :o], u_ref[:o, o:o + b], precision=HI, preferred_element_type=jnp.float32)
        xs_ref[:, o:o + b] = lax.dot_general(
            y, inv_ref[k], (((1,), (1,)), ((), ())), precision=HI, preferred_element_type=jnp.float32)
    x_ref[...] = xs_ref[...].astype(x_ref.dtype)


def factor_solve(tiles, forecast, total, block=128):
    n = forecast.shape[1]
    m = forecast.shape[0]
    vmem = pl.BlockSpec(memory_space=pltpu.VMEM)
    return pl.pallas_call(
        functools.partial(factor_kernel, float(total)),
        out_shape=(jax.ShapeDtypeStruct((m, n), jnp.bfloat16), jax.ShapeDtypeStruct((n, n), jnp.float32)),
        in_specs=[vmem, vmem],
        out_specs=(vmem, vmem),
        scratch_shapes=[
            pltpu.VMEM((n, n), jnp.float32),
            pltpu.VMEM((n // block, block, block), jnp.float32),
            pltpu.VMEM((m, n), jnp.float32),
        ],
    )(tiles, forecast)


def shifted(block, axis, distance):
    devices = range(lax.axis_size(axis))
    route = [(i - distance, i) for i in devices if i - distance in devices]
    return lax.ppermute(block, axis, route)


def doubling_sum(block, axis):
    size = lax.axis_size(axis)
    distance = 1
    while distance < size:
        route = [(i, i ^ distance) for i in range(size)]
        block = block + lax.ppermute(block, axis, route)
        distance *= 2
    return block


def reduce_tiles(tiles):
    count = tiles.shape[0]
    if lax.axis_size("ty") != 2 or count % 2:
        return doubling_sum(doubling_sum(tiles, "tx"), "ty")
    half = count // 2
    side = lax.axis_index("ty")
    swap = [(0, 1), (1, 0)]
    sent = lax.dynamic_slice_in_dim(tiles, (1 - side) * half, half, axis=0)
    kept = lax.dynamic_slice_in_dim(tiles, side * half, half, axis=0)
    kept = kept + lax.ppermute(sent, "ty", swap)
    kept = doubling_sum(kept, "tx")
    other = lax.ppermute(kept, "ty", swap)
    return jnp.where(side == 0, jnp.concatenate([kept, other]), jnp.concatenate([other, kept]))


def group_levels():
    levels = []
    for axis, width in (("ty", 1), ("tx", 2)):
        size = lax.axis_size(axis)
        if size & (size - 1):
            return None
        stride = 1
        while stride < size:
            bits = min(width, (size // stride).bit_length() - 1)
            levels.append((axis, size, stride, 2 ** bits))
            stride *= 2 ** bits
    return levels


def grouped_sum(flat):
    levels = group_levels()
    if levels is None:
        return doubling_sum(doubling_sum(flat, "tx"), "ty")
    pieces = 1
    for level in levels:
        pieces *= level[3]
    if flat.shape[0] % pieces:
        return doubling_sum(doubling_sum(flat, "tx"), "ty")
    digits = []
    for axis, size, stride, group in levels:
        digit = lax.axis_index(axis) // stride % group
        chunk = flat.shape[0] // group
        kept = lax.dynamic_slice_in_dim(flat, digit * chunk, chunk)
        for offset in range(1, group):
            route = [(i, i ^ (offset * stride)) for i in range(size)]
            sent = lax.dynamic_slice_in_dim(flat, (digit ^ offset) * chunk, chunk)
            kept = kept + lax.ppermute(sent, axis, route)
        flat = kept
        digits.append(digit)
    for (axis, size, stride, group), digit in reversed(list(zip(levels, digits))):
        got = [flat]
        for offset in range(1, group):
            route = [(i, i ^ (offset * stride)) for i in range(size)]
            got.append(lax.ppermute(flat, axis, route))
        placed = []
        for position in range(group):
            pick = got[0]
            for offset in range(1, group):
                pick = jnp.where((digit ^ offset) == position, got[offset], pick)
            placed.append(pick)
        flat = jnp.concatenate(placed)
    return flat


def apply_kernel(rows_ref, cols_ref, jac_ref, root_ref, base_ref, *refs):
    out_refs = refs[:-1]
    acc_ref = refs[-1]
    nblk = root_ref.shape[0]
    rim = out_refs[0].shape[0]
    acc_ref[...] = jnp.zeros(acc_ref.shape, jnp.float32)

    def step(n, carry):
        slot = rows_ref[n]
        acc_ref[slot] = acc_ref[slot] + jnp.dot(
            jac_ref[n], root_ref[cols_ref[n]], preferred_element_type=jnp.float32)
        return carry

    lax.fori_loop(0, jac_ref.shape[0], step, 0, unroll=True)
    base_ref[...] = root_ref[...].astype(jnp.float32) + acc_ref[:nblk]
    for k, out_ref in enumerate(out_refs):
        out_ref[...] = acc_ref[nblk + k * rim:nblk + (k + 1) * rim]


def apply_blocks(jac_rows, jac_cols, jac_blocks, root_blocks, slot_count):
    nblk, block, width = root_blocks.shape
    rim = (slot_count - nblk) // 4
    smem = pl.BlockSpec(memory_space=pltpu.SMEM)
    vmem = pl.BlockSpec(memory_space=pltpu.VMEM)
    return pl.pallas_call(
        apply_kernel,
        out_shape=(jax.ShapeDtypeStruct((nblk, block, width), jnp.float32),)
        + tuple(jax.ShapeDtypeStruct((rim, block, width), jnp.float32) for _ in range(4)),
        in_specs=[smem, smem, vmem, vmem],
        out_specs=(vmem,) * 5,
        scratch_shapes=[pltpu.VMEM((slot_count, block, width), jnp.float32)],
    )(jac_rows, jac_cols, jac_blocks, root_blocks)


def land_kernel(landing_ref, base_ref, *refs):
    pieces = refs[:4]
    forecast_ref, tiles_ref, acc_ref = refs[4:]
    nblk, block, width = base_ref.shape
    rim = pieces[0].shape[0]
    acc_ref[...] = base_ref[...]
    for k in range(4):
        for h in range(rim):
            target = landing_ref[k * rim + h]
            acc_ref[target] = acc_ref[target] + pieces[k][h]
    for i in range(nblk):
        forecast_ref[i * block:(i + 1) * block, :] = acc_ref[i]
    whole = forecast_ref[...]
    gram = lax.dot_general(whole, whole, (((0,), (0,)), ((), ())), precision=HI,
                           preferred_element_type=jnp.float32)
    tiles = width // block
    t = 0
    for a in range(tiles):
        for b in range(a, tiles):
            tiles_ref[t] = gram[a * block:(a + 1) * block, b * block:(b + 1) * block]
            t += 1


def land_and_gram(landing, base, pieces):
    nblk, block, width = base.shape
    tiles = width // block
    count = tiles * (tiles + 1) // 2
    smem = pl.BlockSpec(memory_space=pltpu.SMEM)
    vmem = pl.BlockSpec(memory_space=pltpu.VMEM)
    return pl.pallas_call(
        land_kernel,
        out_shape=(
            jax.ShapeDtypeStruct((nblk * block, width), jnp.float32),
            jax.ShapeDtypeStruct((count, block, block), jnp.float32),
        ),
        in_specs=[smem, vmem] + [vmem] * len(pieces),
        out_specs=(vmem, vmem),
        scratch_shapes=[pltpu.VMEM((nblk, block, width), jnp.float32)],
    )(landing, base, *pieces)

def per_device(jac_blocks, jac_rows, jac_cols, landing, covariance_root):
    nnz, block, _ = jac_blocks.shape
    state_rows, mode_columns = covariance_root.shape
    nblk = state_rows // block
    rim = landing.shape[0] // 4
    slot_count = nblk + 4 * rim
    blocks = covariance_root.reshape(nblk, block, mode_columns)
    base, to_prev_x, to_next_x, to_prev_y, to_next_y = apply_blocks(
        jac_rows, jac_cols, jac_blocks, blocks, slot_count)
    from_next_x = shifted(to_prev_x, "tx", -1)
    from_prev_x = shifted(to_next_x, "tx", 1)
    from_next_y = shifted(to_prev_y, "ty", -1)
    from_prev_y = shifted(to_next_y, "ty", 1)
    predicted_root, local_tiles = land_and_gram(
        landing, base, [from_next_x, from_prev_x, from_next_y, from_prev_y])
    total_rows = state_rows * lax.axis_size("tx") * lax.axis_size("ty")
    tiles = mode_columns // block
    upper_sum = grouped_sum(local_tiles.reshape(-1)).reshape(local_tiles.shape)
    rescaled_orthogonal_root, r_factor = factor_solve(upper_sum, predicted_root, total_rows, block)
    return (rescaled_orthogonal_root, r_factor)


def solution(mesh):
    placed = (
        P(("basin", "tx", "ty"), None, None),
        P(("basin", "tx", "ty")),
        P(("basin", "tx", "ty")),
        P(("basin", "tx", "ty")),
        P(("basin", "tx", "ty"), None),
    )
    return jax.shard_map(
        per_device,
        mesh=mesh,
        in_specs=placed,
        out_specs=(P(("basin", "tx", "ty"), None), P("basin", None)),
        check_vma=False,
    )
```

```python
import functools

import jax
import jax.numpy as jnp
from jax import lax
from jax.experimental import pallas as pl
from jax.experimental.pallas import tpu as pltpu
from jax.sharding import PartitionSpec as P

HI = lax.Precision.HIGHEST


def factor_kernel(total, g_ref, f_ref, x_ref, u_ref, w_ref, inv_ref, xs_ref):
    n = f_ref.shape[1]
    b = inv_ref.shape[1]
    nb = n // b
    t = 0
    for first in range(nb):
        for second in range(first, nb):
            tile = g_ref[t] / total
            w_ref[first * b:(first + 1) * b, second * b:(second + 1) * b] = tile
            if second > first:
                w_ref[second * b:(second + 1) * b, first * b:(first + 1) * b] = tile.T
            t += 1
    u_ref[...] = jnp.zeros(u_ref.shape, jnp.float32)
    lane = lax.broadcasted_iota(jnp.int32, (1, b), 1)
    rows = lax.broadcasted_iota(jnp.int32, (b, 1), 0)
    eye = jnp.where(lax.broadcasted_iota(jnp.int32, (b, b), 0) == lax.broadcasted_iota(jnp.int32, (b, b), 1), 1.0, 0.0)
    for k in range(nb):
        o = k * b
        inv_ref[k] = eye
        for j in range(b):
            r = w_ref[o + j:o + j + 1, o:o + b]
            rs = lax.rsqrt(r[:, j:j + 1])
            u = jnp.where(lane >= j, r, 0.0) * rs
            u_ref[o + j:o + j + 1, o:o + b] = u
            brow = inv_ref[k, j:j + 1, :] * rs
            inv_ref[k, j:j + 1, :] = brow
            if j == b - 1:
                break
            s = (j + 1) // 8 * 8
            v = w_ref[o + s:o + b, o + j:o + j + 1] * rs
            v = jnp.where(rows[s:] > j, v, 0.0)
            w_ref[o + s:o + b, o:o + b] = w_ref[o + s:o + b, o:o + b] - v * u
            inv_ref[k, s:, :] = inv_ref[k, s:, :] - v * brow
        if k < nb - 1:
            e = o + b
            panel = jnp.dot(inv_ref[k], w_ref[o:e, e:], precision=HI, preferred_element_type=jnp.float32)
            u_ref[o:e, e:] = panel
            w_ref[e:, e:] = w_ref[e:, e:] - lax.dot_general(
                panel, panel, (((0,), (0,)), ((), ())), precision=HI, preferred_element_type=jnp.float32)
    for k in range(nb):
        o = k * b
        y = f_ref[:, o:o + b]
        if k > 0:
            y = y - jnp.dot(xs_ref[:, :o], u_ref[:o, o:o + b], precision=HI, preferred_element_type=jnp.float32)
        xs_ref[:, o:o + b] = lax.dot_general(
            y, inv_ref[k], (((1,), (1,)), ((), ())), precision=HI, preferred_element_type=jnp.float32)
    x_ref[...] = xs_ref[...].astype(x_ref.dtype)


def factor_solve(tiles, forecast, total, block=128):
    n = forecast.shape[1]
    m = forecast.shape[0]
    vmem = pl.BlockSpec(memory_space=pltpu.VMEM)
    return pl.pallas_call(
        functools.partial(factor_kernel, float(total)),
        out_shape=(jax.ShapeDtypeStruct((m, n), jnp.bfloat16), jax.ShapeDtypeStruct((n, n), jnp.float32)),
        in_specs=[vmem, vmem],
        out_specs=(vmem, vmem),
        scratch_shapes=[
            pltpu.VMEM((n, n), jnp.float32),
            pltpu.VMEM((n // block, block, block), jnp.float32),
            pltpu.VMEM((m, n), jnp.float32),
        ],
    )(tiles, forecast)


def shifted(block, axis, distance):
    devices = range(lax.axis_size(axis))
    route = [(i - distance, i) for i in devices if i - distance in devices]
    return lax.ppermute(block, axis, route)


def doubling_sum(block, axis):
    size = lax.axis_size(axis)
    distance = 1
    while distance < size:
        route = [(i, i ^ distance) for i in range(size)]
        block = block + lax.ppermute(block, axis, route)
        distance *= 2
    return block


def reduce_tiles(tiles):
    count = tiles.shape[0]
    if lax.axis_size("ty") != 2 or count % 2:
        return doubling_sum(doubling_sum(tiles, "tx"), "ty")
    half = count // 2
    side = lax.axis_index("ty")
    swap = [(0, 1), (1, 0)]
    sent = lax.dynamic_slice_in_dim(tiles, (1 - side) * half, half, axis=0)
    kept = lax.dynamic_slice_in_dim(tiles, side * half, half, axis=0)
    kept = kept + lax.ppermute(sent, "ty", swap)
    kept = doubling_sum(kept, "tx")
    other = lax.ppermute(kept, "ty", swap)
    return jnp.where(side == 0, jnp.concatenate([kept, other]), jnp.concatenate([other, kept]))


def group_levels():
    levels = []
    for axis, width in (("ty", 1), ("tx", 2)):
        size = lax.axis_size(axis)
        if size & (size - 1):
            return None
        stride = 1
        while stride < size:
            bits = min(width, (size // stride).bit_length() - 1)
            levels.append((axis, size, stride, 2 ** bits))
            stride *= 2 ** bits
    return levels


def grouped_sum(flat):
    levels = group_levels()
    if levels is None:
        return doubling_sum(doubling_sum(flat, "tx"), "ty")
    pieces = 1
    for level in levels:
        pieces *= level[3]
    if flat.shape[0] % pieces:
        return doubling_sum(doubling_sum(flat, "tx"), "ty")
    digits = []
    for axis, size, stride, group in levels:
        digit = lax.axis_index(axis) // stride % group
        chunk = flat.shape[0] // group
        kept = lax.dynamic_slice_in_dim(flat, digit * chunk, chunk)
        for offset in range(1, group):
            route = [(i, i ^ (offset * stride)) for i in range(size)]
            sent = lax.dynamic_slice_in_dim(flat, (digit ^ offset) * chunk, chunk)
            kept = kept + lax.ppermute(sent, axis, route)
        flat = kept
        digits.append(digit)
    for (axis, size, stride, group), digit in reversed(list(zip(levels, digits))):
        got = [flat]
        for offset in range(1, group):
            route = [(i, i ^ (offset * stride)) for i in range(size)]
            got.append(lax.ppermute(flat, axis, route))
        placed = []
        for position in range(group):
            pick = got[0]
            for offset in range(1, group):
                pick = jnp.where((digit ^ offset) == position, got[offset], pick)
            placed.append(pick)
        flat = jnp.concatenate(placed)
    return flat


def apply_kernel(rows_ref, cols_ref, jac_ref, root_ref, base_ref, *refs):
    out_refs = refs[:-1]
    acc_ref = refs[-1]
    nblk = root_ref.shape[0]
    rim = out_refs[0].shape[0]
    acc_ref[...] = jnp.zeros(acc_ref.shape, jnp.float32)

    def step(n, carry):
        slot = rows_ref[n]
        acc_ref[slot] = acc_ref[slot] + jnp.dot(
            jac_ref[n], root_ref[cols_ref[n]], preferred_element_type=jnp.float32)
        return carry

    lax.fori_loop(0, jac_ref.shape[0], step, 0, unroll=True)
    base_ref[...] = root_ref[...].astype(jnp.float32) + acc_ref[:nblk]
    for k, out_ref in enumerate(out_refs):
        out_ref[...] = acc_ref[nblk + k * rim:nblk + (k + 1) * rim]


def apply_blocks(jac_rows, jac_cols, jac_blocks, root_blocks, slot_count):
    nblk, block, width = root_blocks.shape
    rim = (slot_count - nblk) // 4
    smem = pl.BlockSpec(memory_space=pltpu.SMEM)
    vmem = pl.BlockSpec(memory_space=pltpu.VMEM)
    return pl.pallas_call(
        apply_kernel,
        out_shape=(jax.ShapeDtypeStruct((nblk, block, width), jnp.float32),)
        + tuple(jax.ShapeDtypeStruct((rim, block, width), jnp.float32) for _ in range(4)),
        in_specs=[smem, smem, vmem, vmem],
        out_specs=(vmem,) * 5,
        scratch_shapes=[pltpu.VMEM((slot_count, block, width), jnp.float32)],
    )(jac_rows, jac_cols, jac_blocks, root_blocks)


def land_kernel(landing_ref, base_ref, *refs):
    pieces = refs[:4]
    forecast_ref, tiles_ref, acc_ref = refs[4:]
    nblk, block, width = base_ref.shape
    rim = pieces[0].shape[0]
    acc_ref[...] = base_ref[...]
    for k in range(4):
        for h in range(rim):
            target = landing_ref[k * rim + h]
            acc_ref[target] = acc_ref[target] + pieces[k][h]
    for i in range(nblk):
        forecast_ref[i * block:(i + 1) * block, :] = acc_ref[i]
    whole = forecast_ref[...]
    gram = lax.dot_general(whole, whole, (((0,), (0,)), ((), ())), precision=HI,
                           preferred_element_type=jnp.float32)
    tiles = width // block
    t = 0
    for a in range(tiles):
        for b in range(a, tiles):
            tiles_ref[t] = gram[a * block:(a + 1) * block, b * block:(b + 1) * block]
            t += 1


def land_and_gram(landing, base, pieces):
    nblk, block, width = base.shape
    tiles = width // block
    count = tiles * (tiles + 1) // 2
    smem = pl.BlockSpec(memory_space=pltpu.SMEM)
    vmem = pl.BlockSpec(memory_space=pltpu.VMEM)
    return pl.pallas_call(
        land_kernel,
        out_shape=(
            jax.ShapeDtypeStruct((nblk * block, width), jnp.float32),
            jax.ShapeDtypeStruct((count, block, block), jnp.float32),
        ),
        in_specs=[smem, vmem] + [vmem] * len(pieces),
        out_specs=(vmem, vmem),
        scratch_shapes=[pltpu.VMEM((nblk, block, width), jnp.float32)],
    )(landing, base, *pieces)

def per_device(jac_blocks, jac_rows, jac_cols, landing, covariance_root):
    nnz, block, _ = jac_blocks.shape
    state_rows, mode_columns = covariance_root.shape
    nblk = state_rows // block
    rim = landing.shape[0] // 4
    slot_count = nblk + 4 * rim
    blocks = covariance_root.reshape(nblk, block, mode_columns)
    base, to_prev_x, to_next_x, to_prev_y, to_next_y = apply_blocks(
        jac_rows, jac_cols, jac_blocks, blocks, slot_count)
    from_next_x = shifted(to_prev_x, "tx", -1)
    from_prev_x = shifted(to_next_x, "tx", 1)
    from_next_y = shifted(to_prev_y, "ty", -1)
    from_prev_y = shifted(to_next_y, "ty", 1)
    predicted_root, local_tiles = land_and_gram(
        landing, base, [from_next_x, from_prev_x, from_next_y, from_prev_y])
    total_rows = state_rows * lax.axis_size("tx") * lax.axis_size("ty")
    tiles = mode_columns // block
    upper_sum = grouped_sum(local_tiles.reshape(-1, block)).reshape(local_tiles.shape)
    rescaled_orthogonal_root, r_factor = factor_solve(upper_sum, predicted_root, total_rows, block)
    return (rescaled_orthogonal_root, r_factor)


def solution(mesh):
    placed = (
        P(("basin", "tx", "ty"), None, None),
        P(("basin", "tx", "ty")),
        P(("basin", "tx", "ty")),
        P(("basin", "tx", "ty")),
        P(("basin", "tx", "ty"), None),
    )
    return jax.shard_map(
        per_device,
        mesh=mesh,
        in_specs=placed,
        out_specs=(P(("basin", "tx", "ty"), None), P("basin", None)),
        check_vma=False,
    )
```

```python
import functools

import jax
import jax.numpy as jnp
from jax import lax
from jax.experimental import pallas as pl
from jax.experimental.pallas import tpu as pltpu
from jax.sharding import PartitionSpec as P

HI = lax.Precision.HIGHEST


def factor_kernel(total, g_ref, f_ref, x_ref, u_ref, w_ref, inv_ref, xs_ref):
    n = f_ref.shape[1]
    b = inv_ref.shape[1]
    nb = n // b
    t = 0
    for first in range(nb):
        for second in range(first, nb):
            tile = g_ref[t] / total
            w_ref[first * b:(first + 1) * b, second * b:(second + 1) * b] = tile
            if second > first:
                w_ref[second * b:(second + 1) * b, first * b:(first + 1) * b] = tile.T
            t += 1
    u_ref[...] = jnp.zeros(u_ref.shape, jnp.float32)
    lane = lax.broadcasted_iota(jnp.int32, (1, b), 1)
    rows = lax.broadcasted_iota(jnp.int32, (b, 1), 0)
    eye = jnp.where(lax.broadcasted_iota(jnp.int32, (b, b), 0) == lax.broadcasted_iota(jnp.int32, (b, b), 1), 1.0, 0.0)
    for k in range(nb):
        o = k * b
        inv_ref[k] = eye
        for j in range(b):
            r = w_ref[o + j:o + j + 1, o:o + b]
            rs = lax.rsqrt(r[:, j:j + 1])
            u = jnp.where(lane >= j, r, 0.0) * rs
            u_ref[o + j:o + j + 1, o:o + b] = u
            brow = inv_ref[k, j:j + 1, :] * rs
            inv_ref[k, j:j + 1, :] = brow
            if j == b - 1:
                break
            s = (j + 1) // 8 * 8
            v = w_ref[o + s:o + b, o + j:o + j + 1] * rs
            v = jnp.where(rows[s:] > j, v, 0.0)
            w_ref[o + s:o + b, o:o + b] = w_ref[o + s:o + b, o:o + b] - v * u
            inv_ref[k, s:, :] = inv_ref[k, s:, :] - v * brow
        if k < nb - 1:
            e = o + b
            dims = (((0,), (0,)), ((), ()))
            panel = jnp.dot(inv_ref[k], w_ref[o:e, e:], precision=HI, preferred_element_type=jnp.float32)
            u_ref[o:e, e:] = panel
            near = panel[:, :b]
            w_ref[e:e + b, e:e + b] = w_ref[e:e + b, e:e + b] - lax.dot_general(
                near, near, dims, precision=HI, preferred_element_type=jnp.float32)
            if e + b < n:
                far = panel[:, b:]
                w_ref[e:e + b, e + b:] = w_ref[e:e + b, e + b:] - lax.dot_general(
                    near, far, dims, precision=HI, preferred_element_type=jnp.float32)
                w_ref[e + b:, e + b:] = w_ref[e + b:, e + b:] - lax.dot_general(
                    far, far, dims, precision=HI, preferred_element_type=jnp.float32)
        y = f_ref[:, o:o + b]
        if k > 0:
            y = y - jnp.dot(xs_ref[:, :o], u_ref[:o, o:o + b], precision=HI, preferred_element_type=jnp.float32)
        xs_ref[:, o:o + b] = lax.dot_general(
            y, inv_ref[k], (((1,), (1,)), ((), ())), precision=HI, preferred_element_type=jnp.float32)
    x_ref[...] = xs_ref[...].astype(x_ref.dtype)


def factor_solve(tiles, forecast, total, block=128):
    n = forecast.shape[1]
    m = forecast.shape[0]
    vmem = pl.BlockSpec(memory_space=pltpu.VMEM)
    return pl.pallas_call(
        functools.partial(factor_kernel, float(total)),
        out_shape=(jax.ShapeDtypeStruct((m, n), jnp.bfloat16), jax.ShapeDtypeStruct((n, n), jnp.float32)),
        in_specs=[vmem, vmem],
        out_specs=(vmem, vmem),
        scratch_shapes=[
            pltpu.VMEM((n, n), jnp.float32),
            pltpu.VMEM((n // block, block, block), jnp.float32),
            pltpu.VMEM((m, n), jnp.float32),
        ],
    )(tiles, forecast)


def shifted(block, axis, distance):
    devices = range(lax.axis_size(axis))
    route = [(i - distance, i) for i in devices if i - distance in devices]
    return lax.ppermute(block, axis, route)


def doubling_sum(block, axis):
    size = lax.axis_size(axis)
    distance = 1
    while distance < size:
        route = [(i, i ^ distance) for i in range(size)]
        block = block + lax.ppermute(block, axis, route)
        distance *= 2
    return block


def reduce_tiles(tiles):
    count = tiles.shape[0]
    if lax.axis_size("ty") != 2 or count % 2:
        return doubling_sum(doubling_sum(tiles, "tx"), "ty")
    half = count // 2
    side = lax.axis_index("ty")
    swap = [(0, 1), (1, 0)]
    sent = lax.dynamic_slice_in_dim(tiles, (1 - side) * half, half, axis=0)
    kept = lax.dynamic_slice_in_dim(tiles, side * half, half, axis=0)
    kept = kept + lax.ppermute(sent, "ty", swap)
    kept = doubling_sum(kept, "tx")
    other = lax.ppermute(kept, "ty", swap)
    return jnp.where(side == 0, jnp.concatenate([kept, other]), jnp.concatenate([other, kept]))


def group_levels():
    levels = []
    for axis, width in (("ty", 1), ("tx", 2)):
        size = lax.axis_size(axis)
        if size & (size - 1):
            return None
        stride = 1
        while stride < size:
            bits = min(width, (size // stride).bit_length() - 1)
            levels.append((axis, size, stride, 2 ** bits))
            stride *= 2 ** bits
    return levels


def grouped_sum(flat):
    levels = group_levels()
    if levels is None:
        return doubling_sum(doubling_sum(flat, "tx"), "ty")
    pieces = 1
    for level in levels:
        pieces *= level[3]
    if flat.shape[0] % pieces:
        return doubling_sum(doubling_sum(flat, "tx"), "ty")
    digits = []
    for axis, size, stride, group in levels:
        digit = lax.axis_index(axis) // stride % group
        chunk = flat.shape[0] // group
        kept = lax.dynamic_slice_in_dim(flat, digit * chunk, chunk)
        for offset in range(1, group):
            route = [(i, i ^ (offset * stride)) for i in range(size)]
            sent = lax.dynamic_slice_in_dim(flat, (digit ^ offset) * chunk, chunk)
            kept = kept + lax.ppermute(sent, axis, route)
        flat = kept
        digits.append(digit)
    for (axis, size, stride, group), digit in reversed(list(zip(levels, digits))):
        got = [flat]
        for offset in range(1, group):
            route = [(i, i ^ (offset * stride)) for i in range(size)]
            got.append(lax.ppermute(flat, axis, route))
        placed = []
        for position in range(group):
            pick = got[0]
            for offset in range(1, group):
                pick = jnp.where((digit ^ offset) == position, got[offset], pick)
            placed.append(pick)
        flat = jnp.concatenate(placed)
    return flat


def apply_kernel(rows_ref, cols_ref, jac_ref, root_ref, base_ref, *refs):
    out_refs = refs[:-1]
    acc_ref = refs[-1]
    nblk = root_ref.shape[0]
    rim = out_refs[0].shape[0]
    acc_ref[...] = jnp.zeros(acc_ref.shape, jnp.float32)

    def step(n, carry):
        slot = rows_ref[n]
        acc_ref[slot] = acc_ref[slot] + jnp.dot(
            jac_ref[n], root_ref[cols_ref[n]], preferred_element_type=jnp.float32)
        return carry

    lax.fori_loop(0, jac_ref.shape[0], step, 0, unroll=True)
    base_ref[...] = root_ref[...].astype(jnp.float32) + acc_ref[:nblk]
    for k, out_ref in enumerate(out_refs):
        out_ref[...] = acc_ref[nblk + k * rim:nblk + (k + 1) * rim]


def apply_blocks(jac_rows, jac_cols, jac_blocks, root_blocks, slot_count):
    nblk, block, width = root_blocks.shape
    rim = (slot_count - nblk) // 4
    smem = pl.BlockSpec(memory_space=pltpu.SMEM)
    vmem = pl.BlockSpec(memory_space=pltpu.VMEM)
    return pl.pallas_call(
        apply_kernel,
        out_shape=(jax.ShapeDtypeStruct((nblk, block, width), jnp.float32),)
        + tuple(jax.ShapeDtypeStruct((rim, block, width), jnp.float32) for _ in range(4)),
        in_specs=[smem, smem, vmem, vmem],
        out_specs=(vmem,) * 5,
        scratch_shapes=[pltpu.VMEM((slot_count, block, width), jnp.float32)],
    )(jac_rows, jac_cols, jac_blocks, root_blocks)


def land_kernel(landing_ref, base_ref, *refs):
    pieces = refs[:4]
    forecast_ref, tiles_ref, acc_ref = refs[4:]
    nblk, block, width = base_ref.shape
    rim = pieces[0].shape[0]
    acc_ref[...] = base_ref[...]
    for k in range(4):
        for h in range(rim):
            target = landing_ref[k * rim + h]
            acc_ref[target] = acc_ref[target] + pieces[k][h]
    for i in range(nblk):
        forecast_ref[i * block:(i + 1) * block, :] = acc_ref[i]
    whole = forecast_ref[...]
    gram = lax.dot_general(whole, whole, (((0,), (0,)), ((), ())), precision=HI,
                           preferred_element_type=jnp.float32)
    tiles = width // block
    t = 0
    for a in range(tiles):
        for b in range(a, tiles):
            tiles_ref[t] = gram[a * block:(a + 1) * block, b * block:(b + 1) * block]
            t += 1


def land_and_gram(landing, base, pieces):
    nblk, block, width = base.shape
    tiles = width // block
    count = tiles * (tiles + 1) // 2
    smem = pl.BlockSpec(memory_space=pltpu.SMEM)
    vmem = pl.BlockSpec(memory_space=pltpu.VMEM)
    return pl.pallas_call(
        land_kernel,
        out_shape=(
            jax.ShapeDtypeStruct((nblk * block, width), jnp.float32),
            jax.ShapeDtypeStruct((count, block, block), jnp.float32),
        ),
        in_specs=[smem, vmem] + [vmem] * len(pieces),
        out_specs=(vmem, vmem),
        scratch_shapes=[pltpu.VMEM((nblk, block, width), jnp.float32)],
    )(landing, base, *pieces)

def per_device(jac_blocks, jac_rows, jac_cols, landing, covariance_root):
    nnz, block, _ = jac_blocks.shape
    state_rows, mode_columns = covariance_root.shape
    nblk = state_rows // block
    rim = landing.shape[0] // 4
    slot_count = nblk + 4 * rim
    blocks = covariance_root.reshape(nblk, block, mode_columns)
    base, to_prev_x, to_next_x, to_prev_y, to_next_y = apply_blocks(
        jac_rows, jac_cols, jac_blocks, blocks, slot_count)
    from_next_x = shifted(to_prev_x, "tx", -1)
    from_prev_x = shifted(to_next_x, "tx", 1)
    from_next_y = shifted(to_prev_y, "ty", -1)
    from_prev_y = shifted(to_next_y, "ty", 1)
    predicted_root, local_tiles = land_and_gram(
        landing, base, [from_next_x, from_prev_x, from_next_y, from_prev_y])
    total_rows = state_rows * lax.axis_size("tx") * lax.axis_size("ty")
    tiles = mode_columns // block
    upper_sum = grouped_sum(local_tiles.reshape(-1, block)).reshape(local_tiles.shape)
    rescaled_orthogonal_root, r_factor = factor_solve(upper_sum, predicted_root, total_rows, block)
    return (rescaled_orthogonal_root, r_factor)


def solution(mesh):
    placed = (
        P(("basin", "tx", "ty"), None, None),
        P(("basin", "tx", "ty")),
        P(("basin", "tx", "ty")),
        P(("basin", "tx", "ty")),
        P(("basin", "tx", "ty"), None),
    )
    return jax.shard_map(
        per_device,
        mesh=mesh,
        in_specs=placed,
        out_specs=(P(("basin", "tx", "ty"), None), P("basin", None)),
        check_vma=False,
    )
```

```python
import functools

import jax
import jax.numpy as jnp
from jax import lax
from jax.experimental import pallas as pl
from jax.experimental.pallas import tpu as pltpu
from jax.sharding import PartitionSpec as P

HI = lax.Precision.HIGHEST


def factor_kernel(total, g_ref, f_ref, x_ref, u_ref, w_ref, inv_ref, xs_ref):
    n = f_ref.shape[1]
    b = inv_ref.shape[1]
    nb = n // b
    t = 0
    for first in range(nb):
        for second in range(first, nb):
            tile = g_ref[t] / total
            w_ref[first * b:(first + 1) * b, second * b:(second + 1) * b] = tile
            if second > first:
                w_ref[second * b:(second + 1) * b, first * b:(first + 1) * b] = tile.T
            t += 1
    u_ref[...] = jnp.zeros(u_ref.shape, jnp.float32)
    lane = lax.broadcasted_iota(jnp.int32, (1, b), 1)
    rows = lax.broadcasted_iota(jnp.int32, (b, 1), 0)
    eye = jnp.where(lax.broadcasted_iota(jnp.int32, (b, b), 0) == lax.broadcasted_iota(jnp.int32, (b, b), 1), 1.0, 0.0)
    for k in range(nb):
        o = k * b
        inv_ref[k] = eye
        for j in range(b):
            r = w_ref[o + j:o + j + 1, o:o + b]
            rs = lax.rsqrt(r[:, j:j + 1])
            u = jnp.where(lane >= j, r, 0.0) * rs
            u_ref[o + j:o + j + 1, o:o + b] = u
            brow = inv_ref[k, j:j + 1, :] * rs
            inv_ref[k, j:j + 1, :] = brow
            if j == b - 1:
                break
            s = (j + 1) // 8 * 8
            v = w_ref[o + s:o + b, o + j:o + j + 1] * rs
            v = jnp.where(rows[s:] > j, v, 0.0)
            w_ref[o + s:o + b, o:o + b] = w_ref[o + s:o + b, o:o + b] - v * u
            inv_ref[k, s:, :] = inv_ref[k, s:, :] - v * brow
        if k < nb - 1:
            e = o + b
            dims = (((0,), (0,)), ((), ()))
            panel = jnp.dot(inv_ref[k], w_ref[o:e, e:], precision=HI, preferred_element_type=jnp.float32)
            u_ref[o:e, e:] = panel
            near = panel[:, :b]
            w_ref[e:e + b, e:e + b] = w_ref[e:e + b, e:e + b] - lax.dot_general(
                near, near, dims, precision=HI, preferred_element_type=jnp.float32)
            if e + b < n:
                far = panel[:, b:]
                w_ref[e:e + b, e + b:] = w_ref[e:e + b, e + b:] - lax.dot_general(
                    near, far, dims, precision=HI, preferred_element_type=jnp.float32)
                w_ref[e + b:, e + b:] = w_ref[e + b:, e + b:] - lax.dot_general(
                    far, far, dims, precision=HI, preferred_element_type=jnp.float32)
        y = f_ref[:, o:o + b]
        if k > 0:
            y = y - jnp.dot(xs_ref[:, :o], u_ref[:o, o:o + b], precision=HI, preferred_element_type=jnp.float32)
        xs_ref[:, o:o + b] = lax.dot_general(
            y, inv_ref[k], (((1,), (1,)), ((), ())), precision=HI, preferred_element_type=jnp.float32)
    x_ref[...] = xs_ref[...].astype(x_ref.dtype)


def factor_solve(tiles, forecast, total, block=128):
    n = forecast.shape[1]
    m = forecast.shape[0]
    vmem = pl.BlockSpec(memory_space=pltpu.VMEM)
    return pl.pallas_call(
        functools.partial(factor_kernel, float(total)),
        out_shape=(jax.ShapeDtypeStruct((m, n), jnp.bfloat16), jax.ShapeDtypeStruct((n, n), jnp.float32)),
        in_specs=[vmem, vmem],
        out_specs=(vmem, vmem),
        scratch_shapes=[
            pltpu.VMEM((n, n), jnp.float32),
            pltpu.VMEM((n // block, block, block), jnp.float32),
            pltpu.VMEM((m, n), jnp.float32),
        ],
    )(tiles, forecast)


def shifted(block, axis, distance):
    devices = range(lax.axis_size(axis))
    route = [(i - distance, i) for i in devices if i - distance in devices]
    return lax.ppermute(block, axis, route)


def doubling_sum(block, axis):
    size = lax.axis_size(axis)
    distance = 1
    while distance < size:
        route = [(i, i ^ distance) for i in range(size)]
        block = block + lax.ppermute(block, axis, route)
        distance *= 2
    return block


def reduce_tiles(tiles):
    count = tiles.shape[0]
    if lax.axis_size("ty") != 2 or count % 2:
        return doubling_sum(doubling_sum(tiles, "tx"), "ty")
    half = count // 2
    side = lax.axis_index("ty")
    swap = [(0, 1), (1, 0)]
    sent = lax.dynamic_slice_in_dim(tiles, (1 - side) * half, half, axis=0)
    kept = lax.dynamic_slice_in_dim(tiles, side * half, half, axis=0)
    kept = kept + lax.ppermute(sent, "ty", swap)
    kept = doubling_sum(kept, "tx")
    other = lax.ppermute(kept, "ty", swap)
    return jnp.where(side == 0, jnp.concatenate([kept, other]), jnp.concatenate([other, kept]))


def group_levels():
    levels = []
    for axis, width in (("ty", 1), ("tx", 2)):
        size = lax.axis_size(axis)
        if size & (size - 1):
            return None
        stride = 1
        while stride < size:
            bits = min(width, (size // stride).bit_length() - 1)
            levels.append((axis, size, stride, 2 ** bits))
            stride *= 2 ** bits
    return levels


def grouped_sum(flat):
    levels = group_levels()
    if levels is None:
        return doubling_sum(doubling_sum(flat, "tx"), "ty")
    pieces = 1
    for level in levels:
        pieces *= level[3]
    if flat.shape[0] % pieces:
        return doubling_sum(doubling_sum(flat, "tx"), "ty")
    digits = []
    for axis, size, stride, group in levels:
        digit = lax.axis_index(axis) // stride % group
        chunk = flat.shape[0] // group
        kept = lax.dynamic_slice_in_dim(flat, digit * chunk, chunk)
        for offset in range(1, group):
            route = [(i, i ^ (offset * stride)) for i in range(size)]
            sent = lax.dynamic_slice_in_dim(flat, (digit ^ offset) * chunk, chunk)
            kept = kept + lax.ppermute(sent, axis, route)
        flat = kept
        digits.append(digit)
    for (axis, size, stride, group), digit in reversed(list(zip(levels, digits))):
        got = [flat]
        for offset in range(1, group):
            route = [(i, i ^ (offset * stride)) for i in range(size)]
            got.append(lax.ppermute(flat, axis, route))
        placed = []
        for position in range(group):
            pick = got[0]
            for offset in range(1, group):
                pick = jnp.where((digit ^ offset) == position, got[offset], pick)
            placed.append(pick)
        flat = jnp.concatenate(placed)
    return flat


def apply_kernel(rows_ref, cols_ref, jac_ref, root_ref, base_ref, *refs):
    out_refs = refs[:-1]
    acc_ref = refs[-1]
    nblk = root_ref.shape[0]
    rim = out_refs[0].shape[0]
    acc_ref[...] = jnp.zeros(acc_ref.shape, jnp.float32)

    def step(n, carry):
        slot = rows_ref[n]
        acc_ref[slot] = acc_ref[slot] + jnp.dot(
            jac_ref[n], root_ref[cols_ref[n]], preferred_element_type=jnp.float32)
        return carry

    lax.fori_loop(0, jac_ref.shape[0], step, 0, unroll=True)
    base_ref[...] = root_ref[...].astype(jnp.float32) + acc_ref[:nblk]
    for k, out_ref in enumerate(out_refs):
        out_ref[...] = acc_ref[nblk + k * rim:nblk + (k + 1) * rim]


def apply_blocks(jac_rows, jac_cols, jac_blocks, root_blocks, slot_count):
    nblk, block, width = root_blocks.shape
    rim = (slot_count - nblk) // 4
    smem = pl.BlockSpec(memory_space=pltpu.SMEM)
    vmem = pl.BlockSpec(memory_space=pltpu.VMEM)
    return pl.pallas_call(
        apply_kernel,
        out_shape=(jax.ShapeDtypeStruct((nblk, block, width), jnp.float32),)
        + tuple(jax.ShapeDtypeStruct((rim, block, width), jnp.float32) for _ in range(4)),
        in_specs=[smem, smem, vmem, vmem],
        out_specs=(vmem,) * 5,
        scratch_shapes=[pltpu.VMEM((slot_count, block, width), jnp.float32)],
    )(jac_rows, jac_cols, jac_blocks, root_blocks)


def land_kernel(landing_ref, base_ref, *refs):
    pieces = refs[:4]
    forecast_ref, tiles_ref, acc_ref = refs[4:]
    nblk, block, width = base_ref.shape
    rim = pieces[0].shape[0]
    acc_ref[...] = base_ref[...]
    for k in range(4):
        for h in range(rim):
            target = landing_ref[k * rim + h]
            acc_ref[target] = acc_ref[target] + pieces[k][h]
    for i in range(nblk):
        forecast_ref[i * block:(i + 1) * block, :] = acc_ref[i]
    tiles = width // block
    t = 0
    for a in range(tiles):
        left = forecast_ref[:, a * block:(a + 1) * block]
        right = forecast_ref[:, a * block:]
        band = lax.dot_general(left, right, (((0,), (0,)), ((), ())), precision=HI,
                               preferred_element_type=jnp.float32)
        for b in range(a, tiles):
            tiles_ref[t] = band[:, (b - a) * block:(b - a + 1) * block]
            t += 1


def land_and_gram(landing, base, pieces):
    nblk, block, width = base.shape
    tiles = width // block
    count = tiles * (tiles + 1) // 2
    smem = pl.BlockSpec(memory_space=pltpu.SMEM)
    vmem = pl.BlockSpec(memory_space=pltpu.VMEM)
    return pl.pallas_call(
        land_kernel,
        out_shape=(
            jax.ShapeDtypeStruct((nblk * block, width), jnp.float32),
            jax.ShapeDtypeStruct((count, block, block), jnp.float32),
        ),
        in_specs=[smem, vmem] + [vmem] * len(pieces),
        out_specs=(vmem, vmem),
        scratch_shapes=[pltpu.VMEM((nblk, block, width), jnp.float32)],
    )(landing, base, *pieces)

def per_device(jac_blocks, jac_rows, jac_cols, landing, covariance_root):
    nnz, block, _ = jac_blocks.shape
    state_rows, mode_columns = covariance_root.shape
    nblk = state_rows // block
    rim = landing.shape[0] // 4
    slot_count = nblk + 4 * rim
    blocks = covariance_root.reshape(nblk, block, mode_columns)
    base, to_prev_x, to_next_x, to_prev_y, to_next_y = apply_blocks(
        jac_rows, jac_cols, jac_blocks, blocks, slot_count)
    from_next_x = shifted(to_prev_x, "tx", -1)
    from_prev_x = shifted(to_next_x, "tx", 1)
    from_next_y = shifted(to_prev_y, "ty", -1)
    from_prev_y = shifted(to_next_y, "ty", 1)
    predicted_root, local_tiles = land_and_gram(
        landing, base, [from_next_x, from_prev_x, from_next_y, from_prev_y])
    total_rows = state_rows * lax.axis_size("tx") * lax.axis_size("ty")
    tiles = mode_columns // block
    upper_sum = grouped_sum(local_tiles.reshape(-1, block)).reshape(local_tiles.shape)
    rescaled_orthogonal_root, r_factor = factor_solve(upper_sum, predicted_root, total_rows, block)
    return (rescaled_orthogonal_root, r_factor)


def solution(mesh):
    placed = (
        P(("basin", "tx", "ty"), None, None),
        P(("basin", "tx", "ty")),
        P(("basin", "tx", "ty")),
        P(("basin", "tx", "ty")),
        P(("basin", "tx", "ty"), None),
    )
    return jax.shard_map(
        per_device,
        mesh=mesh,
        in_specs=placed,
        out_specs=(P(("basin", "tx", "ty"), None), P("basin", None)),
        check_vma=False,
    )
```

```python
import functools

import jax
import jax.numpy as jnp
from jax import lax
from jax.experimental import pallas as pl
from jax.experimental.pallas import tpu as pltpu
from jax.sharding import PartitionSpec as P

HI = lax.Precision.HIGHEST


def factor_kernel(total, g_ref, f_ref, x_ref, u_ref, w_ref, inv_ref, xs_ref):
    n = f_ref.shape[1]
    b = inv_ref.shape[1]
    nb = n // b
    t = 0
    for first in range(nb):
        for second in range(first, nb):
            tile = g_ref[t] / total
            w_ref[first * b:(first + 1) * b, second * b:(second + 1) * b] = tile
            t += 1
    for first in range(1, nb):
        w_ref[first * b:, (first - 1) * b:first * b] = jnp.zeros(((nb - first) * b, b), jnp.float32)
    u_ref[...] = jnp.zeros(u_ref.shape, jnp.float32)
    lane = lax.broadcasted_iota(jnp.int32, (1, b), 1)
    rows = lax.broadcasted_iota(jnp.int32, (b, 1), 0)
    eye = jnp.where(lax.broadcasted_iota(jnp.int32, (b, b), 0) == lax.broadcasted_iota(jnp.int32, (b, b), 1), 1.0, 0.0)
    for k in range(nb):
        o = k * b
        inv_ref[k] = eye
        for j in range(b):
            r = w_ref[o + j:o + j + 1, o:o + b]
            rs = lax.rsqrt(r[:, j:j + 1])
            u = jnp.where(lane >= j, r, 0.0) * rs
            u_ref[o + j:o + j + 1, o:o + b] = u
            brow = inv_ref[k, j:j + 1, :] * rs
            inv_ref[k, j:j + 1, :] = brow
            if j == b - 1:
                break
            s = (j + 1) // 8 * 8
            v = w_ref[o + s:o + b, o + j:o + j + 1] * rs
            v = jnp.where(rows[s:] > j, v, 0.0)
            w_ref[o + s:o + b, o:o + b] = w_ref[o + s:o + b, o:o + b] - v * u
            inv_ref[k, s:, :] = inv_ref[k, s:, :] - v * brow
        if k < nb - 1:
            e = o + b
            dims = (((0,), (0,)), ((), ()))
            panel = jnp.dot(inv_ref[k], w_ref[o:e, e:], precision=HI, preferred_element_type=jnp.float32)
            u_ref[o:e, e:] = panel
            near = panel[:, :b]
            w_ref[e:e + b, e:e + b] = w_ref[e:e + b, e:e + b] - lax.dot_general(
                near, near, dims, precision=HI, preferred_element_type=jnp.float32)
            if e + b < n:
                far = panel[:, b:]
                w_ref[e:e + b, e + b:] = w_ref[e:e + b, e + b:] - lax.dot_general(
                    near, far, dims, precision=HI, preferred_element_type=jnp.float32)
                w_ref[e + b:, e + b:] = w_ref[e + b:, e + b:] - lax.dot_general(
                    far, far, dims, precision=HI, preferred_element_type=jnp.float32)
        y = f_ref[:, o:o + b]
        if k > 0:
            y = y - jnp.dot(xs_ref[:, :o], u_ref[:o, o:o + b], precision=HI, preferred_element_type=jnp.float32)
        xs_ref[:, o:o + b] = lax.dot_general(
            y, inv_ref[k], (((1,), (1,)), ((), ())), precision=HI, preferred_element_type=jnp.float32)
    x_ref[...] = xs_ref[...].astype(x_ref.dtype)


def factor_solve(tiles, forecast, total, block=128):
    n = forecast.shape[1]
    m = forecast.shape[0]
    vmem = pl.BlockSpec(memory_space=pltpu.VMEM)
    return pl.pallas_call(
        functools.partial(factor_kernel, float(total)),
        out_shape=(jax.ShapeDtypeStruct((m, n), jnp.bfloat16), jax.ShapeDtypeStruct((n, n), jnp.float32)),
        in_specs=[vmem, vmem],
        out_specs=(vmem, vmem),
        scratch_shapes=[
            pltpu.VMEM((n, n), jnp.float32),
            pltpu.VMEM((n // block, block, block), jnp.float32),
            pltpu.VMEM((m, n), jnp.float32),
        ],
    )(tiles, forecast)


def shifted(block, axis, distance):
    devices = range(lax.axis_size(axis))
    route = [(i - distance, i) for i in devices if i - distance in devices]
    return lax.ppermute(block, axis, route)


def doubling_sum(block, axis):
    size = lax.axis_size(axis)
    distance = 1
    while distance < size:
        route = [(i, i ^ distance) for i in range(size)]
        block = block + lax.ppermute(block, axis, route)
        distance *= 2
    return block


def reduce_tiles(tiles):
    count = tiles.shape[0]
    if lax.axis_size("ty") != 2 or count % 2:
        return doubling_sum(doubling_sum(tiles, "tx"), "ty")
    half = count // 2
    side = lax.axis_index("ty")
    swap = [(0, 1), (1, 0)]
    sent = lax.dynamic_slice_in_dim(tiles, (1 - side) * half, half, axis=0)
    kept = lax.dynamic_slice_in_dim(tiles, side * half, half, axis=0)
    kept = kept + lax.ppermute(sent, "ty", swap)
    kept = doubling_sum(kept, "tx")
    other = lax.ppermute(kept, "ty", swap)
    return jnp.where(side == 0, jnp.concatenate([kept, other]), jnp.concatenate([other, kept]))


def group_levels():
    levels = []
    for axis, width in (("ty", 1), ("tx", 2)):
        size = lax.axis_size(axis)
        if size & (size - 1):
            return None
        stride = 1
        while stride < size:
            bits = min(width, (size // stride).bit_length() - 1)
            levels.append((axis, size, stride, 2 ** bits))
            stride *= 2 ** bits
    return levels


def grouped_sum(flat):
    levels = group_levels()
    if levels is None:
        return doubling_sum(doubling_sum(flat, "tx"), "ty")
    pieces = 1
    for level in levels:
        pieces *= level[3]
    if flat.shape[0] % pieces:
        return doubling_sum(doubling_sum(flat, "tx"), "ty")
    digits = []
    for axis, size, stride, group in levels:
        digit = lax.axis_index(axis) // stride % group
        chunk = flat.shape[0] // group
        kept = lax.dynamic_slice_in_dim(flat, digit * chunk, chunk)
        for offset in range(1, group):
            route = [(i, i ^ (offset * stride)) for i in range(size)]
            sent = lax.dynamic_slice_in_dim(flat, (digit ^ offset) * chunk, chunk)
            kept = kept + lax.ppermute(sent, axis, route)
        flat = kept
        digits.append(digit)
    for (axis, size, stride, group), digit in reversed(list(zip(levels, digits))):
        got = [flat]
        for offset in range(1, group):
            route = [(i, i ^ (offset * stride)) for i in range(size)]
            got.append(lax.ppermute(flat, axis, route))
        placed = []
        for position in range(group):
            pick = got[0]
            for offset in range(1, group):
                pick = jnp.where((digit ^ offset) == position, got[offset], pick)
            placed.append(pick)
        flat = jnp.concatenate(placed)
    return flat


def apply_kernel(rows_ref, cols_ref, jac_ref, root_ref, base_ref, *refs):
    out_refs = refs[:-1]
    acc_ref = refs[-1]
    nblk = root_ref.shape[0]
    rim = out_refs[0].shape[0]
    acc_ref[...] = jnp.zeros(acc_ref.shape, jnp.float32)

    def step(n, carry):
        slot = rows_ref[n]
        acc_ref[slot] = acc_ref[slot] + jnp.dot(
            jac_ref[n], root_ref[cols_ref[n]], preferred_element_type=jnp.float32)
        return carry

    lax.fori_loop(0, jac_ref.shape[0], step, 0, unroll=True)
    base_ref[...] = root_ref[...].astype(jnp.float32) + acc_ref[:nblk]
    for k, out_ref in enumerate(out_refs):
        out_ref[...] = acc_ref[nblk + k * rim:nblk + (k + 1) * rim]


def apply_blocks(jac_rows, jac_cols, jac_blocks, root_blocks, slot_count):
    nblk, block, width = root_blocks.shape
    rim = (slot_count - nblk) // 4
    smem = pl.BlockSpec(memory_space=pltpu.SMEM)
    vmem = pl.BlockSpec(memory_space=pltpu.VMEM)
    return pl.pallas_call(
        apply_kernel,
        out_shape=(jax.ShapeDtypeStruct((nblk, block, width), jnp.float32),)
        + tuple(jax.ShapeDtypeStruct((rim, block, width), jnp.float32) for _ in range(4)),
        in_specs=[smem, smem, vmem, vmem],
        out_specs=(vmem,) * 5,
        scratch_shapes=[pltpu.VMEM((slot_count, block, width), jnp.float32)],
    )(jac_rows, jac_cols, jac_blocks, root_blocks)


def land_kernel(landing_ref, base_ref, *refs):
    pieces = refs[:4]
    forecast_ref, tiles_ref, acc_ref = refs[4:]
    nblk, block, width = base_ref.shape
    rim = pieces[0].shape[0]
    acc_ref[...] = base_ref[...]
    for k in range(4):
        for h in range(rim):
            target = landing_ref[k * rim + h]
            acc_ref[target] = acc_ref[target] + pieces[k][h]
    for i in range(nblk):
        forecast_ref[i * block:(i + 1) * block, :] = acc_ref[i]
    tiles = width // block
    t = 0
    for a in range(tiles):
        left = forecast_ref[:, a * block:(a + 1) * block]
        right = forecast_ref[:, a * block:]
        band = lax.dot_general(left, right, (((0,), (0,)), ((), ())), precision=HI,
                               preferred_element_type=jnp.float32)
        for b in range(a, tiles):
            tiles_ref[t] = band[:, (b - a) * block:(b - a + 1) * block]
            t += 1


def land_and_gram(landing, base, pieces):
    nblk, block, width = base.shape
    tiles = width // block
    count = tiles * (tiles + 1) // 2
    smem = pl.BlockSpec(memory_space=pltpu.SMEM)
    vmem = pl.BlockSpec(memory_space=pltpu.VMEM)
    return pl.pallas_call(
        land_kernel,
        out_shape=(
            jax.ShapeDtypeStruct((nblk * block, width), jnp.float32),
            jax.ShapeDtypeStruct((count, block, block), jnp.float32),
        ),
        in_specs=[smem, vmem] + [vmem] * len(pieces),
        out_specs=(vmem, vmem),
        scratch_shapes=[pltpu.VMEM((nblk, block, width), jnp.float32)],
    )(landing, base, *pieces)

def per_device(jac_blocks, jac_rows, jac_cols, landing, covariance_root):
    nnz, block, _ = jac_blocks.shape
    state_rows, mode_columns = covariance_root.shape
    nblk = state_rows // block
    rim = landing.shape[0] // 4
    slot_count = nblk + 4 * rim
    blocks = covariance_root.reshape(nblk, block, mode_columns)
    base, to_prev_x, to_next_x, to_prev_y, to_next_y = apply_blocks(
        jac_rows, jac_cols, jac_blocks, blocks, slot_count)
    from_next_x = shifted(to_prev_x, "tx", -1)
    from_prev_x = shifted(to_next_x, "tx", 1)
    from_next_y = shifted(to_prev_y, "ty", -1)
    from_prev_y = shifted(to_next_y, "ty", 1)
    predicted_root, local_tiles = land_and_gram(
        landing, base, [from_next_x, from_prev_x, from_next_y, from_prev_y])
    total_rows = state_rows * lax.axis_size("tx") * lax.axis_size("ty")
    tiles = mode_columns // block
    upper_sum = grouped_sum(local_tiles.reshape(-1, block)).reshape(local_tiles.shape)
    rescaled_orthogonal_root, r_factor = factor_solve(upper_sum, predicted_root, total_rows, block)
    return (rescaled_orthogonal_root, r_factor)


def solution(mesh):
    placed = (
        P(("basin", "tx", "ty"), None, None),
        P(("basin", "tx", "ty")),
        P(("basin", "tx", "ty")),
        P(("basin", "tx", "ty")),
        P(("basin", "tx", "ty"), None),
    )
    return jax.shard_map(
        per_device,
        mesh=mesh,
        in_specs=placed,
        out_specs=(P(("basin", "tx", "ty"), None), P("basin", None)),
        check_vma=False,
    )
```

```python
import functools

import jax
import jax.numpy as jnp
from jax import lax
from jax.experimental import pallas as pl
from jax.experimental.pallas import tpu as pltpu
from jax.sharding import PartitionSpec as P

HI = lax.Precision.HIGHEST


def factor_kernel(total, g_ref, f_ref, x_ref, u_ref, w_ref, inv_ref, xs_ref):
    n = f_ref.shape[1]
    b = inv_ref.shape[1]
    nb = n // b
    t = 0
    for first in range(nb):
        for second in range(first, nb):
            tile = g_ref[t] / total
            w_ref[first * b:(first + 1) * b, second * b:(second + 1) * b] = tile
            if second > first:
                w_ref[second * b:(second + 1) * b, first * b:(first + 1) * b] = tile.T
            t += 1
    u_ref[...] = jnp.zeros(u_ref.shape, jnp.float32)
    lane = lax.broadcasted_iota(jnp.int32, (1, b), 1)
    rows = lax.broadcasted_iota(jnp.int32, (b, 1), 0)
    eye = jnp.where(lax.broadcasted_iota(jnp.int32, (b, b), 0) == lax.broadcasted_iota(jnp.int32, (b, b), 1), 1.0, 0.0)
    for k in range(nb):
        o = k * b
        inv_ref[k] = eye
        for j in range(b):
            r = w_ref[o + j:o + j + 1, o:o + b]
            rs = lax.rsqrt(r[:, j:j + 1])
            u = jnp.where(lane >= j, r, 0.0) * rs
            u_ref[o + j:o + j + 1, o:o + b] = u
            brow = inv_ref[k, j:j + 1, :] * rs
            inv_ref[k, j:j + 1, :] = brow
            if j == b - 1:
                break
            s = (j + 1) // 8 * 8
            v = w_ref[o + s:o + b, o + j:o + j + 1] * rs
            v = jnp.where(rows[s:] > j, v, 0.0)
            w_ref[o + s:o + b, o:o + b] = w_ref[o + s:o + b, o:o + b] - v * u
            inv_ref[k, s:, :] = inv_ref[k, s:, :] - v * brow
        if k < nb - 1:
            e = o + b
            dims = (((0,), (0,)), ((), ()))
            panel = jnp.dot(inv_ref[k], w_ref[o:e, e:], precision=HI, preferred_element_type=jnp.float32)
            u_ref[o:e, e:] = panel
            near = panel[:, :b]
            w_ref[e:e + b, e:e + b] = w_ref[e:e + b, e:e + b] - lax.dot_general(
                near, near, dims, precision=HI, preferred_element_type=jnp.float32)
            if e + b < n:
                far = panel[:, b:]
                w_ref[e:e + b, e + b:] = w_ref[e:e + b, e + b:] - lax.dot_general(
                    near, far, dims, precision=HI, preferred_element_type=jnp.float32)
                w_ref[e + b:, e + b:] = w_ref[e + b:, e + b:] - lax.dot_general(
                    far, far, dims, precision=HI, preferred_element_type=jnp.float32)
        y = f_ref[:, o:o + b]
        if k > 0:
            y = y - jnp.dot(xs_ref[:, :o], u_ref[:o, o:o + b], precision=HI, preferred_element_type=jnp.float32)
        xs_ref[:, o:o + b] = lax.dot_general(
            y, inv_ref[k], (((1,), (1,)), ((), ())), precision=HI, preferred_element_type=jnp.float32)
    x_ref[...] = xs_ref[...].astype(x_ref.dtype)


def factor_solve(tiles, forecast, total, block=128):
    n = forecast.shape[1]
    m = forecast.shape[0]
    vmem = pl.BlockSpec(memory_space=pltpu.VMEM)
    return pl.pallas_call(
        functools.partial(factor_kernel, float(total)),
        out_shape=(jax.ShapeDtypeStruct((m, n), jnp.bfloat16), jax.ShapeDtypeStruct((n, n), jnp.float32)),
        in_specs=[vmem, vmem],
        out_specs=(vmem, vmem),
        scratch_shapes=[
            pltpu.VMEM((n, n), jnp.float32),
            pltpu.VMEM((n // block, block, block), jnp.float32),
            pltpu.VMEM((m, n), jnp.float32),
        ],
    )(tiles, forecast)


def shifted(block, axis, distance):
    devices = range(lax.axis_size(axis))
    route = [(i - distance, i) for i in devices if i - distance in devices]
    return lax.ppermute(block, axis, route)


def doubling_sum(block, axis):
    size = lax.axis_size(axis)
    distance = 1
    while distance < size:
        route = [(i, i ^ distance) for i in range(size)]
        block = block + lax.ppermute(block, axis, route)
        distance *= 2
    return block


def reduce_tiles(tiles):
    count = tiles.shape[0]
    if lax.axis_size("ty") != 2 or count % 2:
        return doubling_sum(doubling_sum(tiles, "tx"), "ty")
    half = count // 2
    side = lax.axis_index("ty")
    swap = [(0, 1), (1, 0)]
    sent = lax.dynamic_slice_in_dim(tiles, (1 - side) * half, half, axis=0)
    kept = lax.dynamic_slice_in_dim(tiles, side * half, half, axis=0)
    kept = kept + lax.ppermute(sent, "ty", swap)
    kept = doubling_sum(kept, "tx")
    other = lax.ppermute(kept, "ty", swap)
    return jnp.where(side == 0, jnp.concatenate([kept, other]), jnp.concatenate([other, kept]))


def group_levels():
    levels = []
    for axis, width in (("ty", 1), ("tx", 2)):
        size = lax.axis_size(axis)
        if size & (size - 1):
            return None
        stride = 1
        while stride < size:
            bits = min(width, (size // stride).bit_length() - 1)
            levels.append((axis, size, stride, 2 ** bits))
            stride *= 2 ** bits
    return levels


def grouped_sum(flat, rolled=False):
    levels = group_levels()
    if levels is None:
        return doubling_sum(doubling_sum(flat, "tx"), "ty")
    pieces = 1
    for level in levels:
        pieces *= level[3]
    if flat.shape[0] % pieces:
        return doubling_sum(doubling_sum(flat, "tx"), "ty")
    digits = []
    for axis, size, stride, group in levels:
        digit = lax.axis_index(axis) // stride % group
        chunk = flat.shape[0] // group
        if rolled and not digits:
            kept = flat[:chunk] + lax.ppermute(flat[chunk:], axis, [(i, i ^ stride) for i in range(size)])
            flat = kept
            digits.append(digit)
            continue
        kept = lax.dynamic_slice_in_dim(flat, digit * chunk, chunk)
        for offset in range(1, group):
            route = [(i, i ^ (offset * stride)) for i in range(size)]
            sent = lax.dynamic_slice_in_dim(flat, (digit ^ offset) * chunk, chunk)
            kept = kept + lax.ppermute(sent, axis, route)
        flat = kept
        digits.append(digit)
    for (axis, size, stride, group), digit in reversed(list(zip(levels, digits))):
        got = [flat]
        for offset in range(1, group):
            route = [(i, i ^ (offset * stride)) for i in range(size)]
            got.append(lax.ppermute(flat, axis, route))
        placed = []
        for position in range(group):
            pick = got[0]
            for offset in range(1, group):
                pick = jnp.where((digit ^ offset) == position, got[offset], pick)
            placed.append(pick)
        flat = jnp.concatenate(placed)
    return flat


def apply_kernel(rows_ref, cols_ref, jac_ref, root_ref, base_ref, *refs):
    out_refs = refs[:-1]
    acc_ref = refs[-1]
    nblk = root_ref.shape[0]
    rim = out_refs[0].shape[0]
    acc_ref[...] = jnp.zeros(acc_ref.shape, jnp.float32)

    def step(n, carry):
        slot = rows_ref[n]
        acc_ref[slot] = acc_ref[slot] + jnp.dot(
            jac_ref[n], root_ref[cols_ref[n]], preferred_element_type=jnp.float32)
        return carry

    lax.fori_loop(0, jac_ref.shape[0], step, 0, unroll=True)
    base_ref[...] = root_ref[...].astype(jnp.float32) + acc_ref[:nblk]
    for k, out_ref in enumerate(out_refs):
        out_ref[...] = acc_ref[nblk + k * rim:nblk + (k + 1) * rim]


def apply_blocks(jac_rows, jac_cols, jac_blocks, root_blocks, slot_count):
    nblk, block, width = root_blocks.shape
    rim = (slot_count - nblk) // 4
    smem = pl.BlockSpec(memory_space=pltpu.SMEM)
    vmem = pl.BlockSpec(memory_space=pltpu.VMEM)
    return pl.pallas_call(
        apply_kernel,
        out_shape=(jax.ShapeDtypeStruct((nblk, block, width), jnp.float32),)
        + tuple(jax.ShapeDtypeStruct((rim, block, width), jnp.float32) for _ in range(4)),
        in_specs=[smem, smem, vmem, vmem],
        out_specs=(vmem,) * 5,
        scratch_shapes=[pltpu.VMEM((slot_count, block, width), jnp.float32)],
    )(jac_rows, jac_cols, jac_blocks, root_blocks)


def land_kernel(landing_ref, shift_ref, base_ref, *refs):
    pieces = refs[:4]
    forecast_ref, tiles_ref, acc_ref = refs[4:]
    nblk, block, width = base_ref.shape
    rim = pieces[0].shape[0]
    acc_ref[...] = base_ref[...]
    for k in range(4):
        for h in range(rim):
            target = landing_ref[k * rim + h]
            acc_ref[target] = acc_ref[target] + pieces[k][h]
    for i in range(nblk):
        forecast_ref[i * block:(i + 1) * block, :] = acc_ref[i]
    tiles = width // block
    t = 0
    for a in range(tiles):
        left = forecast_ref[:, a * block:(a + 1) * block]
        right = forecast_ref[:, a * block:]
        band = lax.dot_general(left, right, (((0,), (0,)), ((), ())), precision=HI,
                               preferred_element_type=jnp.float32)
        for b in range(a, tiles):
            tiles_ref[(t + shift_ref[0]) % tiles_ref.shape[0]] = band[:, (b - a) * block:(b - a + 1) * block]
            t += 1


def land_and_gram(landing, shift, base, pieces):
    nblk, block, width = base.shape
    tiles = width // block
    count = tiles * (tiles + 1) // 2
    smem = pl.BlockSpec(memory_space=pltpu.SMEM)
    vmem = pl.BlockSpec(memory_space=pltpu.VMEM)
    return pl.pallas_call(
        land_kernel,
        out_shape=(
            jax.ShapeDtypeStruct((nblk * block, width), jnp.float32),
            jax.ShapeDtypeStruct((count, block, block), jnp.float32),
        ),
        in_specs=[smem, smem, vmem] + [vmem] * len(pieces),
        out_specs=(vmem, vmem),
        scratch_shapes=[pltpu.VMEM((nblk, block, width), jnp.float32)],
    )(landing, shift, base, *pieces)

def per_device(jac_blocks, jac_rows, jac_cols, landing, covariance_root):
    nnz, block, _ = jac_blocks.shape
    state_rows, mode_columns = covariance_root.shape
    nblk = state_rows // block
    rim = landing.shape[0] // 4
    slot_count = nblk + 4 * rim
    blocks = covariance_root.reshape(nblk, block, mode_columns)
    base, to_prev_x, to_next_x, to_prev_y, to_next_y = apply_blocks(
        jac_rows, jac_cols, jac_blocks, blocks, slot_count)
    from_next_x = shifted(to_prev_x, "tx", -1)
    from_prev_x = shifted(to_next_x, "tx", 1)
    from_next_y = shifted(to_prev_y, "ty", -1)
    from_prev_y = shifted(to_next_y, "ty", 1)
    tiles = mode_columns // block
    count = tiles * (tiles + 1) // 2
    levels = group_levels()
    rolled = bool(levels) and levels[0][0] == "ty" and levels[0][3] == 2 and count % 2 == 0
    shift = lax.axis_index("ty") * (count // 2) if rolled else 0
    shift = jnp.full((1,), shift, jnp.int32)
    predicted_root, local_tiles = land_and_gram(
        landing, shift, base, [from_next_x, from_prev_x, from_next_y, from_prev_y])
    total_rows = state_rows * lax.axis_size("tx") * lax.axis_size("ty")
    tiles = mode_columns // block
    upper_sum = grouped_sum(local_tiles.reshape(-1, block), rolled).reshape(local_tiles.shape)
    rescaled_orthogonal_root, r_factor = factor_solve(upper_sum, predicted_root, total_rows, block)
    return (rescaled_orthogonal_root, r_factor)


def solution(mesh):
    placed = (
        P(("basin", "tx", "ty"), None, None),
        P(("basin", "tx", "ty")),
        P(("basin", "tx", "ty")),
        P(("basin", "tx", "ty")),
        P(("basin", "tx", "ty"), None),
    )
    return jax.shard_map(
        per_device,
        mesh=mesh,
        in_specs=placed,
        out_specs=(P(("basin", "tx", "ty"), None), P("basin", None)),
        check_vma=False,
    )
```

```python
import functools

import jax
import jax.numpy as jnp
from jax import lax
from jax.experimental import pallas as pl
from jax.experimental.pallas import tpu as pltpu
from jax.sharding import PartitionSpec as P

HI = lax.Precision.HIGHEST


def factor_kernel(total, g_ref, f_ref, x_ref, u_ref, w_ref, inv_ref, xs_ref):
    n = f_ref.shape[1]
    b = inv_ref.shape[1]
    nb = n // b
    t = 0
    for first in range(nb):
        for second in range(first, nb):
            tile = g_ref[t] / total
            w_ref[first * b:(first + 1) * b, second * b:(second + 1) * b] = tile
            if second > first:
                w_ref[second * b:(second + 1) * b, first * b:(first + 1) * b] = tile.T
            t += 1
    u_ref[...] = jnp.zeros(u_ref.shape, jnp.float32)
    lane = lax.broadcasted_iota(jnp.int32, (1, b), 1)
    rows = lax.broadcasted_iota(jnp.int32, (b, 1), 0)
    eye = jnp.where(lax.broadcasted_iota(jnp.int32, (b, b), 0) == lax.broadcasted_iota(jnp.int32, (b, b), 1), 1.0, 0.0)
    for k in range(nb):
        o = k * b
        inv_ref[k] = eye
        for j in range(b):
            r = w_ref[o + j:o + j + 1, o:o + b]
            rs = lax.rsqrt(r[:, j:j + 1])
            u = jnp.where(lane >= j, r, 0.0) * rs
            u_ref[o + j:o + j + 1, o:o + b] = u
            brow = inv_ref[k, j:j + 1, :] * rs
            inv_ref[k, j:j + 1, :] = brow
            if j == b - 1:
                break
            s = (j + 1) // 8 * 8
            v = w_ref[o + s:o + b, o + j:o + j + 1] * rs
            v = jnp.where(rows[s:] > j, v, 0.0)
            w_ref[o + s:o + b, o:o + b] = w_ref[o + s:o + b, o:o + b] - v * u
            inv_ref[k, s:, :] = inv_ref[k, s:, :] - v * brow
        if k < nb - 1:
            e = o + b
            dims = (((0,), (0,)), ((), ()))
            panel = jnp.dot(inv_ref[k], w_ref[o:e, e:], precision=HI, preferred_element_type=jnp.float32)
            u_ref[o:e, e:] = panel
            near = panel[:, :b]
            w_ref[e:e + b, e:e + b] = w_ref[e:e + b, e:e + b] - lax.dot_general(
                near, near, dims, precision=HI, preferred_element_type=jnp.float32)
            if e + b < n:
                far = panel[:, b:]
                w_ref[e:e + b, e + b:] = w_ref[e:e + b, e + b:] - lax.dot_general(
                    near, far, dims, precision=HI, preferred_element_type=jnp.float32)
                w_ref[e + b:, e + b:] = w_ref[e + b:, e + b:] - lax.dot_general(
                    far, far, dims, precision=HI, preferred_element_type=jnp.float32)
        y = f_ref[:, o:o + b]
        if k > 0:
            y = y - jnp.dot(xs_ref[:, :o], u_ref[:o, o:o + b], precision=HI, preferred_element_type=jnp.float32)
        xs_ref[:, o:o + b] = lax.dot_general(
            y, inv_ref[k], (((1,), (1,)), ((), ())), precision=HI, preferred_element_type=jnp.float32)
    x_ref[...] = xs_ref[...].astype(x_ref.dtype)


def factor_solve(tiles, forecast, total, block=128):
    n = forecast.shape[1]
    m = forecast.shape[0]
    vmem = pl.BlockSpec(memory_space=pltpu.VMEM)
    return pl.pallas_call(
        functools.partial(factor_kernel, float(total)),
        out_shape=(jax.ShapeDtypeStruct((m, n), jnp.bfloat16), jax.ShapeDtypeStruct((n, n), jnp.float32)),
        in_specs=[vmem, vmem],
        out_specs=(vmem, vmem),
        scratch_shapes=[
            pltpu.VMEM((n, n), jnp.float32),
            pltpu.VMEM((n // block, block, block), jnp.float32),
            pltpu.VMEM((m, n), jnp.float32),
        ],
    )(tiles, forecast)


def shifted(block, axis, distance):
    devices = range(lax.axis_size(axis))
    route = [(i - distance, i) for i in devices if i - distance in devices]
    return lax.ppermute(block, axis, route)


def doubling_sum(block, axis):
    size = lax.axis_size(axis)
    distance = 1
    while distance < size:
        route = [(i, i ^ distance) for i in range(size)]
        block = block + lax.ppermute(block, axis, route)
        distance *= 2
    return block


def reduce_tiles(tiles):
    count = tiles.shape[0]
    if lax.axis_size("ty") != 2 or count % 2:
        return doubling_sum(doubling_sum(tiles, "tx"), "ty")
    half = count // 2
    side = lax.axis_index("ty")
    swap = [(0, 1), (1, 0)]
    sent = lax.dynamic_slice_in_dim(tiles, (1 - side) * half, half, axis=0)
    kept = lax.dynamic_slice_in_dim(tiles, side * half, half, axis=0)
    kept = kept + lax.ppermute(sent, "ty", swap)
    kept = doubling_sum(kept, "tx")
    other = lax.ppermute(kept, "ty", swap)
    return jnp.where(side == 0, jnp.concatenate([kept, other]), jnp.concatenate([other, kept]))


def group_levels():
    levels = []
    for axis, width in (("ty", 1), ("tx", 2)):
        size = lax.axis_size(axis)
        if size & (size - 1):
            return None
        stride = 1
        while stride < size:
            bits = min(width, (size // stride).bit_length() - 1)
            levels.append((axis, size, stride, 2 ** bits))
            stride *= 2 ** bits
    return levels


def grouped_sum(flat, rolled=False):
    levels = group_levels()
    if rolled:
        head, tail = flat
        side = lax.axis_index("ty")
        flat = jnp.where(side == 0, jnp.concatenate([head, tail]), jnp.concatenate([tail, head]))
    pieces = 1
    for level in levels or ():
        pieces *= level[3]
    if levels is None or flat.shape[0] % pieces:
        return doubling_sum(doubling_sum(flat, "tx"), "ty")
    if rolled:
        flat = head
    digits = []
    for axis, size, stride, group in levels:
        digit = lax.axis_index(axis) // stride % group
        chunk = flat.shape[0] // group
        if rolled and not digits:
            kept = head + lax.ppermute(tail, axis, [(i, i ^ stride) for i in range(size)])
            flat = kept
            digits.append(digit)
            continue
        kept = lax.dynamic_slice_in_dim(flat, digit * chunk, chunk)
        for offset in range(1, group):
            route = [(i, i ^ (offset * stride)) for i in range(size)]
            sent = lax.dynamic_slice_in_dim(flat, (digit ^ offset) * chunk, chunk)
            kept = kept + lax.ppermute(sent, axis, route)
        flat = kept
        digits.append(digit)
    for (axis, size, stride, group), digit in reversed(list(zip(levels, digits))):
        got = [flat]
        for offset in range(1, group):
            route = [(i, i ^ (offset * stride)) for i in range(size)]
            got.append(lax.ppermute(flat, axis, route))
        placed = []
        for position in range(group):
            pick = got[0]
            for offset in range(1, group):
                pick = jnp.where((digit ^ offset) == position, got[offset], pick)
            placed.append(pick)
        flat = jnp.concatenate(placed)
    return flat


def apply_kernel(rows_ref, cols_ref, jac_ref, root_ref, base_ref, *refs):
    out_refs = refs[:-1]
    acc_ref = refs[-1]
    nblk = root_ref.shape[0]
    rim = out_refs[0].shape[0]
    acc_ref[...] = jnp.zeros(acc_ref.shape, jnp.float32)

    def step(n, carry):
        slot = rows_ref[n]
        acc_ref[slot] = acc_ref[slot] + jnp.dot(
            jac_ref[n], root_ref[cols_ref[n]], preferred_element_type=jnp.float32)
        return carry

    lax.fori_loop(0, jac_ref.shape[0], step, 0, unroll=True)
    base_ref[...] = root_ref[...].astype(jnp.float32) + acc_ref[:nblk]
    for k, out_ref in enumerate(out_refs):
        out_ref[...] = acc_ref[nblk + k * rim:nblk + (k + 1) * rim]


def apply_blocks(jac_rows, jac_cols, jac_blocks, root_blocks, slot_count):
    nblk, block, width = root_blocks.shape
    rim = (slot_count - nblk) // 4
    smem = pl.BlockSpec(memory_space=pltpu.SMEM)
    vmem = pl.BlockSpec(memory_space=pltpu.VMEM)
    return pl.pallas_call(
        apply_kernel,
        out_shape=(jax.ShapeDtypeStruct((nblk, block, width), jnp.float32),)
        + tuple(jax.ShapeDtypeStruct((rim, block, width), jnp.float32) for _ in range(4)),
        in_specs=[smem, smem, vmem, vmem],
        out_specs=(vmem,) * 5,
        scratch_shapes=[pltpu.VMEM((slot_count, block, width), jnp.float32)],
    )(jac_rows, jac_cols, jac_blocks, root_blocks)


def land_kernel(landing_ref, shift_ref, base_ref, *refs):
    pieces = refs[:4]
    forecast_ref, kept_ref, sent_ref, acc_ref = refs[4:]
    lead = kept_ref.shape[0]
    count = lead + sent_ref.shape[0]
    nblk, block, width = base_ref.shape
    rim = pieces[0].shape[0]
    acc_ref[...] = base_ref[...]
    for k in range(4):
        for h in range(rim):
            target = landing_ref[k * rim + h]
            acc_ref[target] = acc_ref[target] + pieces[k][h]
    for i in range(nblk):
        forecast_ref[i * block:(i + 1) * block, :] = acc_ref[i]
    tiles = width // block
    t = 0
    for a in range(tiles):
        left = forecast_ref[:, a * block:(a + 1) * block]
        right = forecast_ref[:, a * block:]
        band = lax.dot_general(left, right, (((0,), (0,)), ((), ())), precision=HI,
                               preferred_element_type=jnp.float32)
        for b in range(a, tiles):
            tile = band[:, (b - a) * block:(b - a + 1) * block]
            spot = (t + shift_ref[0]) % count

            @pl.when(spot < lead)
            def _():
                kept_ref[jnp.minimum(spot, lead - 1)] = tile

            @pl.when(spot >= lead)
            def _():
                sent_ref[jnp.maximum(spot - lead, 0)] = tile

            t += 1


def land_and_gram(landing, shift, base, pieces):
    nblk, block, width = base.shape
    tiles = width // block
    count = tiles * (tiles + 1) // 2
    smem = pl.BlockSpec(memory_space=pltpu.SMEM)
    vmem = pl.BlockSpec(memory_space=pltpu.VMEM)
    return pl.pallas_call(
        land_kernel,
        out_shape=(
            jax.ShapeDtypeStruct((nblk * block, width), jnp.float32),
            jax.ShapeDtypeStruct(((count + 1) // 2, block, block), jnp.float32),
            jax.ShapeDtypeStruct((count // 2, block, block), jnp.float32),
        ),
        in_specs=[smem, smem, vmem] + [vmem] * len(pieces),
        out_specs=(vmem, vmem, vmem),
        scratch_shapes=[pltpu.VMEM((nblk, block, width), jnp.float32)],
    )(landing, shift, base, *pieces)

def per_device(jac_blocks, jac_rows, jac_cols, landing, covariance_root):
    nnz, block, _ = jac_blocks.shape
    state_rows, mode_columns = covariance_root.shape
    nblk = state_rows // block
    rim = landing.shape[0] // 4
    slot_count = nblk + 4 * rim
    blocks = covariance_root.reshape(nblk, block, mode_columns)
    base, to_prev_x, to_next_x, to_prev_y, to_next_y = apply_blocks(
        jac_rows, jac_cols, jac_blocks, blocks, slot_count)
    from_next_x = shifted(to_prev_x, "tx", -1)
    from_prev_x = shifted(to_next_x, "tx", 1)
    from_next_y = shifted(to_prev_y, "ty", -1)
    from_prev_y = shifted(to_next_y, "ty", 1)
    tiles = mode_columns // block
    count = tiles * (tiles + 1) // 2
    levels = group_levels()
    rolled = bool(levels) and levels[0][0] == "ty" and levels[0][3] == 2 and count % 2 == 0
    shift = lax.axis_index("ty") * (count // 2) if rolled else 0
    shift = jnp.full((1,), shift, jnp.int32)
    predicted_root, kept_tiles, sent_tiles = land_and_gram(
        landing, shift, base, [from_next_x, from_prev_x, from_next_y, from_prev_y])
    local_tiles = (kept_tiles, sent_tiles) if rolled else jnp.concatenate([kept_tiles, sent_tiles])
    total_rows = state_rows * lax.axis_size("tx") * lax.axis_size("ty")
    tiles = mode_columns // block
    if rolled:
        flat = tuple(part.reshape(-1, block) for part in local_tiles)
    else:
        flat = local_tiles.reshape(-1, block)
    upper_sum = grouped_sum(flat, rolled).reshape(count, block, block)
    rescaled_orthogonal_root, r_factor = factor_solve(upper_sum, predicted_root, total_rows, block)
    return (rescaled_orthogonal_root, r_factor)


def solution(mesh):
    placed = (
        P(("basin", "tx", "ty"), None, None),
        P(("basin", "tx", "ty")),
        P(("basin", "tx", "ty")),
        P(("basin", "tx", "ty")),
        P(("basin", "tx", "ty"), None),
    )
    return jax.shard_map(
        per_device,
        mesh=mesh,
        in_specs=placed,
        out_specs=(P(("basin", "tx", "ty"), None), P("basin", None)),
        check_vma=False,
    )
```

```python
import functools

import jax
import jax.numpy as jnp
from jax import lax
from jax.experimental import pallas as pl
from jax.experimental.pallas import tpu as pltpu
from jax.sharding import PartitionSpec as P

HI = lax.Precision.HIGHEST


def fill_gram(w_ref, halves, total, nb, b):
    lead = halves[0].shape[0]
    t = 0
    for first in range(nb):
        for second in range(first, nb):
            tile = halves[t // lead][t % lead] / total
            w_ref[first * b:(first + 1) * b, second * b:(second + 1) * b] = tile
            if second > first:
                w_ref[second * b:(second + 1) * b, first * b:(first + 1) * b] = tile.T
            t += 1


def factor_kernel(total, side_ref, g_ref, h_ref, f_ref, x_ref, u_ref, w_ref, inv_ref, xs_ref):
    n = f_ref.shape[1]
    b = inv_ref.shape[1]
    nb = n // b

    @pl.when(side_ref[0] == 0)
    def _():
        fill_gram(w_ref, (g_ref, h_ref), total, nb, b)

    @pl.when(side_ref[0] != 0)
    def _():
        fill_gram(w_ref, (h_ref, g_ref), total, nb, b)

    u_ref[...] = jnp.zeros(u_ref.shape, jnp.float32)
    lane = lax.broadcasted_iota(jnp.int32, (1, b), 1)
    rows = lax.broadcasted_iota(jnp.int32, (b, 1), 0)
    eye = jnp.where(lax.broadcasted_iota(jnp.int32, (b, b), 0) == lax.broadcasted_iota(jnp.int32, (b, b), 1), 1.0, 0.0)
    for k in range(nb):
        o = k * b
        inv_ref[k] = eye
        for j in range(b):
            r = w_ref[o + j:o + j + 1, o:o + b]
            rs = lax.rsqrt(r[:, j:j + 1])
            u = jnp.where(lane >= j, r, 0.0) * rs
            u_ref[o + j:o + j + 1, o:o + b] = u
            brow = inv_ref[k, j:j + 1, :] * rs
            inv_ref[k, j:j + 1, :] = brow
            if j == b - 1:
                break
            s = (j + 1) // 8 * 8
            v = w_ref[o + s:o + b, o + j:o + j + 1] * rs
            v = jnp.where(rows[s:] > j, v, 0.0)
            w_ref[o + s:o + b, o:o + b] = w_ref[o + s:o + b, o:o + b] - v * u
            inv_ref[k, s:, :] = inv_ref[k, s:, :] - v * brow
        if k < nb - 1:
            e = o + b
            dims = (((0,), (0,)), ((), ()))
            panel = jnp.dot(inv_ref[k], w_ref[o:e, e:], precision=HI, preferred_element_type=jnp.float32)
            u_ref[o:e, e:] = panel
            near = panel[:, :b]
            w_ref[e:e + b, e:e + b] = w_ref[e:e + b, e:e + b] - lax.dot_general(
                near, near, dims, precision=HI, preferred_element_type=jnp.float32)
            if e + b < n:
                far = panel[:, b:]
                w_ref[e:e + b, e + b:] = w_ref[e:e + b, e + b:] - lax.dot_general(
                    near, far, dims, precision=HI, preferred_element_type=jnp.float32)
                w_ref[e + b:, e + b:] = w_ref[e + b:, e + b:] - lax.dot_general(
                    far, far, dims, precision=HI, preferred_element_type=jnp.float32)
        y = f_ref[:, o:o + b]
        if k > 0:
            y = y - jnp.dot(xs_ref[:, :o], u_ref[:o, o:o + b], precision=HI, preferred_element_type=jnp.float32)
        xs_ref[:, o:o + b] = lax.dot_general(
            y, inv_ref[k], (((1,), (1,)), ((), ())), precision=HI, preferred_element_type=jnp.float32)
    x_ref[...] = xs_ref[...].astype(x_ref.dtype)


def factor_solve(side, kept, other, forecast, total, block=128):
    n = forecast.shape[1]
    m = forecast.shape[0]
    vmem = pl.BlockSpec(memory_space=pltpu.VMEM)
    return pl.pallas_call(
        functools.partial(factor_kernel, float(total)),
        out_shape=(jax.ShapeDtypeStruct((m, n), jnp.bfloat16), jax.ShapeDtypeStruct((n, n), jnp.float32)),
        in_specs=[pl.BlockSpec(memory_space=pltpu.SMEM), vmem, vmem, vmem],
        out_specs=(vmem, vmem),
        scratch_shapes=[
            pltpu.VMEM((n, n), jnp.float32),
            pltpu.VMEM((n // block, block, block), jnp.float32),
            pltpu.VMEM((m, n), jnp.float32),
        ],
    )(side, kept, other, forecast)


def shifted(block, axis, distance):
    devices = range(lax.axis_size(axis))
    route = [(i - distance, i) for i in devices if i - distance in devices]
    return lax.ppermute(block, axis, route)


def doubling_sum(block, axis):
    size = lax.axis_size(axis)
    distance = 1
    while distance < size:
        route = [(i, i ^ distance) for i in range(size)]
        block = block + lax.ppermute(block, axis, route)
        distance *= 2
    return block


def reduce_tiles(tiles):
    count = tiles.shape[0]
    if lax.axis_size("ty") != 2 or count % 2:
        return doubling_sum(doubling_sum(tiles, "tx"), "ty")
    half = count // 2
    side = lax.axis_index("ty")
    swap = [(0, 1), (1, 0)]
    sent = lax.dynamic_slice_in_dim(tiles, (1 - side) * half, half, axis=0)
    kept = lax.dynamic_slice_in_dim(tiles, side * half, half, axis=0)
    kept = kept + lax.ppermute(sent, "ty", swap)
    kept = doubling_sum(kept, "tx")
    other = lax.ppermute(kept, "ty", swap)
    return jnp.where(side == 0, jnp.concatenate([kept, other]), jnp.concatenate([other, kept]))


def group_levels():
    levels = []
    for axis, width in (("ty", 1), ("tx", 2)):
        size = lax.axis_size(axis)
        if size & (size - 1):
            return None
        stride = 1
        while stride < size:
            bits = min(width, (size // stride).bit_length() - 1)
            levels.append((axis, size, stride, 2 ** bits))
            stride *= 2 ** bits
    return levels


def grouped_sum(flat, split=False):
    levels = group_levels()
    if levels is None:
        return doubling_sum(doubling_sum(flat, "tx"), "ty")
    pieces = 1
    for level in levels:
        pieces *= level[3]
    if flat.shape[0] % pieces:
        return doubling_sum(doubling_sum(flat, "tx"), "ty")
    digits = []
    for axis, size, stride, group in levels:
        digit = lax.axis_index(axis) // stride % group
        chunk = flat.shape[0] // group
        kept = lax.dynamic_slice_in_dim(flat, digit * chunk, chunk)
        for offset in range(1, group):
            route = [(i, i ^ (offset * stride)) for i in range(size)]
            sent = lax.dynamic_slice_in_dim(flat, (digit ^ offset) * chunk, chunk)
            kept = kept + lax.ppermute(sent, axis, route)
        flat = kept
        digits.append(digit)
    for depth, ((axis, size, stride, group), digit) in reversed(list(enumerate(zip(levels, digits)))):
        got = [flat]
        for offset in range(1, group):
            route = [(i, i ^ (offset * stride)) for i in range(size)]
            got.append(lax.ppermute(flat, axis, route))
        if split and depth == 0 and group == 2:
            return got[0], got[1], digit
        placed = []
        for position in range(group):
            pick = got[0]
            for offset in range(1, group):
                pick = jnp.where((digit ^ offset) == position, got[offset], pick)
            placed.append(pick)
        flat = jnp.concatenate(placed)
    return flat


def apply_kernel(rows_ref, cols_ref, jac_ref, root_ref, base_ref, *refs):
    out_refs = refs[:-1]
    acc_ref = refs[-1]
    nblk = root_ref.shape[0]
    rim = out_refs[0].shape[0]
    acc_ref[...] = jnp.zeros(acc_ref.shape, jnp.float32)

    def step(n, carry):
        slot = rows_ref[n]
        acc_ref[slot] = acc_ref[slot] + jnp.dot(
            jac_ref[n], root_ref[cols_ref[n]], preferred_element_type=jnp.float32)
        return carry

    lax.fori_loop(0, jac_ref.shape[0], step, 0, unroll=True)
    base_ref[...] = root_ref[...].astype(jnp.float32) + acc_ref[:nblk]
    for k, out_ref in enumerate(out_refs):
        out_ref[...] = acc_ref[nblk + k * rim:nblk + (k + 1) * rim]


def apply_blocks(jac_rows, jac_cols, jac_blocks, root_blocks, slot_count):
    nblk, block, width = root_blocks.shape
    rim = (slot_count - nblk) // 4
    smem = pl.BlockSpec(memory_space=pltpu.SMEM)
    vmem = pl.BlockSpec(memory_space=pltpu.VMEM)
    return pl.pallas_call(
        apply_kernel,
        out_shape=(jax.ShapeDtypeStruct((nblk, block, width), jnp.float32),)
        + tuple(jax.ShapeDtypeStruct((rim, block, width), jnp.float32) for _ in range(4)),
        in_specs=[smem, smem, vmem, vmem],
        out_specs=(vmem,) * 5,
        scratch_shapes=[pltpu.VMEM((slot_count, block, width), jnp.float32)],
    )(jac_rows, jac_cols, jac_blocks, root_blocks)


def land_kernel(landing_ref, base_ref, *refs):
    pieces = refs[:4]
    forecast_ref, tiles_ref, acc_ref = refs[4:]
    nblk, block, width = base_ref.shape
    rim = pieces[0].shape[0]
    acc_ref[...] = base_ref[...]
    for k in range(4):
        for h in range(rim):
            target = landing_ref[k * rim + h]
            acc_ref[target] = acc_ref[target] + pieces[k][h]
    for i in range(nblk):
        forecast_ref[i * block:(i + 1) * block, :] = acc_ref[i]
    tiles = width // block
    t = 0
    for a in range(tiles):
        left = forecast_ref[:, a * block:(a + 1) * block]
        right = forecast_ref[:, a * block:]
        band = lax.dot_general(left, right, (((0,), (0,)), ((), ())), precision=HI,
                               preferred_element_type=jnp.float32)
        for b in range(a, tiles):
            tiles_ref[t] = band[:, (b - a) * block:(b - a + 1) * block]
            t += 1


def land_and_gram(landing, base, pieces):
    nblk, block, width = base.shape
    tiles = width // block
    count = tiles * (tiles + 1) // 2
    smem = pl.BlockSpec(memory_space=pltpu.SMEM)
    vmem = pl.BlockSpec(memory_space=pltpu.VMEM)
    return pl.pallas_call(
        land_kernel,
        out_shape=(
            jax.ShapeDtypeStruct((nblk * block, width), jnp.float32),
            jax.ShapeDtypeStruct((count, block, block), jnp.float32),
        ),
        in_specs=[smem, vmem] + [vmem] * len(pieces),
        out_specs=(vmem, vmem),
        scratch_shapes=[pltpu.VMEM((nblk, block, width), jnp.float32)],
    )(landing, base, *pieces)

def per_device(jac_blocks, jac_rows, jac_cols, landing, covariance_root):
    nnz, block, _ = jac_blocks.shape
    state_rows, mode_columns = covariance_root.shape
    nblk = state_rows // block
    rim = landing.shape[0] // 4
    slot_count = nblk + 4 * rim
    blocks = covariance_root.reshape(nblk, block, mode_columns)
    base, to_prev_x, to_next_x, to_prev_y, to_next_y = apply_blocks(
        jac_rows, jac_cols, jac_blocks, blocks, slot_count)
    from_next_x = shifted(to_prev_x, "tx", -1)
    from_prev_x = shifted(to_next_x, "tx", 1)
    from_next_y = shifted(to_prev_y, "ty", -1)
    from_prev_y = shifted(to_next_y, "ty", 1)
    predicted_root, local_tiles = land_and_gram(
        landing, base, [from_next_x, from_prev_x, from_next_y, from_prev_y])
    total_rows = state_rows * lax.axis_size("tx") * lax.axis_size("ty")
    tiles = mode_columns // block
    levels = group_levels()
    count = local_tiles.shape[0]
    if levels and levels[0][0] == "ty" and levels[0][3] == 2 and count % 2 == 0:
        kept, other, side = grouped_sum(local_tiles.reshape(-1, block), True)
        if isinstance(kept, tuple):
            raise ValueError("unsplit")
    else:
        kept = grouped_sum(local_tiles.reshape(-1, block))
        other = kept[:0]
        side = 0
    kept = kept.reshape(-1, block, block)
    other = other.reshape(-1, block, block)
    side = jnp.full((1,), side, jnp.int32)
    rescaled_orthogonal_root, r_factor = factor_solve(side, kept, other, predicted_root, total_rows, block)
    return (rescaled_orthogonal_root, r_factor)


def solution(mesh):
    placed = (
        P(("basin", "tx", "ty"), None, None),
        P(("basin", "tx", "ty")),
        P(("basin", "tx", "ty")),
        P(("basin", "tx", "ty")),
        P(("basin", "tx", "ty"), None),
    )
    return jax.shard_map(
        per_device,
        mesh=mesh,
        in_specs=placed,
        out_specs=(P(("basin", "tx", "ty"), None), P("basin", None)),
        check_vma=False,
    )
```

```python
import functools

import jax
import jax.numpy as jnp
from jax import lax
from jax.experimental import pallas as pl
from jax.experimental.pallas import tpu as pltpu
from jax.sharding import PartitionSpec as P

HI = lax.Precision.HIGHEST


def factor_kernel(total, g_ref, f_ref, x_ref, u_ref, w_ref, inv_ref, xs_ref):
    n = f_ref.shape[1]
    b = inv_ref.shape[1]
    nb = n // b
    t = 0
    for first in range(nb):
        for second in range(first, nb):
            tile = g_ref[t] / total
            w_ref[first * b:(first + 1) * b, second * b:(second + 1) * b] = tile
            if second > first:
                w_ref[second * b:(second + 1) * b, first * b:(first + 1) * b] = tile.T
            t += 1
    for first in range(1, nb):
        u_ref[first * b:, (first - 1) * b:first * b] = jnp.zeros(((nb - first) * b, b), jnp.float32)
    lane = lax.broadcasted_iota(jnp.int32, (1, b), 1)
    rows = lax.broadcasted_iota(jnp.int32, (b, 1), 0)
    eye = jnp.where(lax.broadcasted_iota(jnp.int32, (b, b), 0) == lax.broadcasted_iota(jnp.int32, (b, b), 1), 1.0, 0.0)
    for k in range(nb):
        o = k * b
        inv_ref[k] = eye
        for j in range(b):
            r = w_ref[o + j:o + j + 1, o:o + b]
            rs = lax.rsqrt(r[:, j:j + 1])
            u = jnp.where(lane >= j, r, 0.0) * rs
            u_ref[o + j:o + j + 1, o:o + b] = u
            brow = inv_ref[k, j:j + 1, :] * rs
            inv_ref[k, j:j + 1, :] = brow
            if j == b - 1:
                break
            s = (j + 1) // 8 * 8
            v = w_ref[o + s:o + b, o + j:o + j + 1] * rs
            v = jnp.where(rows[s:] > j, v, 0.0)
            w_ref[o + s:o + b, o:o + b] = w_ref[o + s:o + b, o:o + b] - v * u
            inv_ref[k, s:, :] = inv_ref[k, s:, :] - v * brow
        if k < nb - 1:
            e = o + b
            dims = (((0,), (0,)), ((), ()))
            panel = jnp.dot(inv_ref[k], w_ref[o:e, e:], precision=HI, preferred_element_type=jnp.float32)
            u_ref[o:e, e:] = panel
            near = panel[:, :b]
            w_ref[e:e + b, e:e + b] = w_ref[e:e + b, e:e + b] - lax.dot_general(
                near, near, dims, precision=HI, preferred_element_type=jnp.float32)
            if e + b < n:
                far = panel[:, b:]
                w_ref[e:e + b, e + b:] = w_ref[e:e + b, e + b:] - lax.dot_general(
                    near, far, dims, precision=HI, preferred_element_type=jnp.float32)
                w_ref[e + b:, e + b:] = w_ref[e + b:, e + b:] - lax.dot_general(
                    far, far, dims, precision=HI, preferred_element_type=jnp.float32)
        y = f_ref[:, o:o + b]
        if k > 0:
            y = y - jnp.dot(xs_ref[:, :o], u_ref[:o, o:o + b], precision=HI, preferred_element_type=jnp.float32)
        xs_ref[:, o:o + b] = lax.dot_general(
            y, inv_ref[k], (((1,), (1,)), ((), ())), precision=HI, preferred_element_type=jnp.float32)
    x_ref[...] = xs_ref[...].astype(x_ref.dtype)


def factor_solve(tiles, forecast, total, block=128):
    n = forecast.shape[1]
    m = forecast.shape[0]
    vmem = pl.BlockSpec(memory_space=pltpu.VMEM)
    return pl.pallas_call(
        functools.partial(factor_kernel, float(total)),
        out_shape=(jax.ShapeDtypeStruct((m, n), jnp.bfloat16), jax.ShapeDtypeStruct((n, n), jnp.float32)),
        in_specs=[vmem, vmem],
        out_specs=(vmem, vmem),
        scratch_shapes=[
            pltpu.VMEM((n, n), jnp.float32),
            pltpu.VMEM((n // block, block, block), jnp.float32),
            pltpu.VMEM((m, n), jnp.float32),
        ],
    )(tiles, forecast)


def shifted(block, axis, distance):
    devices = range(lax.axis_size(axis))
    route = [(i - distance, i) for i in devices if i - distance in devices]
    return lax.ppermute(block, axis, route)


def doubling_sum(block, axis):
    size = lax.axis_size(axis)
    distance = 1
    while distance < size:
        route = [(i, i ^ distance) for i in range(size)]
        block = block + lax.ppermute(block, axis, route)
        distance *= 2
    return block


def reduce_tiles(tiles):
    count = tiles.shape[0]
    if lax.axis_size("ty") != 2 or count % 2:
        return doubling_sum(doubling_sum(tiles, "tx"), "ty")
    half = count // 2
    side = lax.axis_index("ty")
    swap = [(0, 1), (1, 0)]
    sent = lax.dynamic_slice_in_dim(tiles, (1 - side) * half, half, axis=0)
    kept = lax.dynamic_slice_in_dim(tiles, side * half, half, axis=0)
    kept = kept + lax.ppermute(sent, "ty", swap)
    kept = doubling_sum(kept, "tx")
    other = lax.ppermute(kept, "ty", swap)
    return jnp.where(side == 0, jnp.concatenate([kept, other]), jnp.concatenate([other, kept]))


def group_levels():
    levels = []
    for axis, width in (("ty", 1), ("tx", 2)):
        size = lax.axis_size(axis)
        if size & (size - 1):
            return None
        stride = 1
        while stride < size:
            bits = min(width, (size // stride).bit_length() - 1)
            levels.append((axis, size, stride, 2 ** bits))
            stride *= 2 ** bits
    return levels


def grouped_sum(flat):
    levels = group_levels()
    if levels is None:
        return doubling_sum(doubling_sum(flat, "tx"), "ty")
    pieces = 1
    for level in levels:
        pieces *= level[3]
    if flat.shape[0] % pieces:
        return doubling_sum(doubling_sum(flat, "tx"), "ty")
    digits = []
    for axis, size, stride, group in levels:
        digit = lax.axis_index(axis) // stride % group
        chunk = flat.shape[0] // group
        kept = lax.dynamic_slice_in_dim(flat, digit * chunk, chunk)
        for offset in range(1, group):
            route = [(i, i ^ (offset * stride)) for i in range(size)]
            sent = lax.dynamic_slice_in_dim(flat, (digit ^ offset) * chunk, chunk)
            kept = kept + lax.ppermute(sent, axis, route)
        flat = kept
        digits.append(digit)
    for (axis, size, stride, group), digit in reversed(list(zip(levels, digits))):
        got = [flat]
        for offset in range(1, group):
            route = [(i, i ^ (offset * stride)) for i in range(size)]
            got.append(lax.ppermute(flat, axis, route))
        placed = []
        for position in range(group):
            pick = got[0]
            for offset in range(1, group):
                pick = jnp.where((digit ^ offset) == position, got[offset], pick)
            placed.append(pick)
        flat = jnp.concatenate(placed)
    return flat


def apply_kernel(rows_ref, cols_ref, jac_ref, root_ref, base_ref, *refs):
    out_refs = refs[:-1]
    acc_ref = refs[-1]
    nblk = root_ref.shape[0]
    rim = out_refs[0].shape[0]
    acc_ref[...] = jnp.zeros(acc_ref.shape, jnp.float32)

    def step(n, carry):
        slot = rows_ref[n]
        acc_ref[slot] = acc_ref[slot] + jnp.dot(
            jac_ref[n], root_ref[cols_ref[n]], preferred_element_type=jnp.float32)
        return carry

    lax.fori_loop(0, jac_ref.shape[0], step, 0, unroll=True)
    base_ref[...] = root_ref[...].astype(jnp.float32) + acc_ref[:nblk]
    for k, out_ref in enumerate(out_refs):
        out_ref[...] = acc_ref[nblk + k * rim:nblk + (k + 1) * rim]


def apply_blocks(jac_rows, jac_cols, jac_blocks, root_blocks, slot_count):
    nblk, block, width = root_blocks.shape
    rim = (slot_count - nblk) // 4
    smem = pl.BlockSpec(memory_space=pltpu.SMEM)
    vmem = pl.BlockSpec(memory_space=pltpu.VMEM)
    return pl.pallas_call(
        apply_kernel,
        out_shape=(jax.ShapeDtypeStruct((nblk, block, width), jnp.float32),)
        + tuple(jax.ShapeDtypeStruct((rim, block, width), jnp.float32) for _ in range(4)),
        in_specs=[smem, smem, vmem, vmem],
        out_specs=(vmem,) * 5,
        scratch_shapes=[pltpu.VMEM((slot_count, block, width), jnp.float32)],
    )(jac_rows, jac_cols, jac_blocks, root_blocks)


def land_kernel(landing_ref, base_ref, *refs):
    pieces = refs[:4]
    forecast_ref, tiles_ref, acc_ref = refs[4:]
    nblk, block, width = base_ref.shape
    rim = pieces[0].shape[0]
    acc_ref[...] = base_ref[...]
    for k in range(4):
        for h in range(rim):
            target = landing_ref[k * rim + h]
            acc_ref[target] = acc_ref[target] + pieces[k][h]
    for i in range(nblk):
        forecast_ref[i * block:(i + 1) * block, :] = acc_ref[i]
    tiles = width // block
    t = 0
    for a in range(tiles):
        left = forecast_ref[:, a * block:(a + 1) * block]
        right = forecast_ref[:, a * block:]
        band = lax.dot_general(left, right, (((0,), (0,)), ((), ())), precision=HI,
                               preferred_element_type=jnp.float32)
        for b in range(a, tiles):
            tiles_ref[t] = band[:, (b - a) * block:(b - a + 1) * block]
            t += 1


def land_and_gram(landing, base, pieces):
    nblk, block, width = base.shape
    tiles = width // block
    count = tiles * (tiles + 1) // 2
    smem = pl.BlockSpec(memory_space=pltpu.SMEM)
    vmem = pl.BlockSpec(memory_space=pltpu.VMEM)
    return pl.pallas_call(
        land_kernel,
        out_shape=(
            jax.ShapeDtypeStruct((nblk * block, width), jnp.float32),
            jax.ShapeDtypeStruct((count, block, block), jnp.float32),
        ),
        in_specs=[smem, vmem] + [vmem] * len(pieces),
        out_specs=(vmem, vmem),
        scratch_shapes=[pltpu.VMEM((nblk, block, width), jnp.float32)],
    )(landing, base, *pieces)

def per_device(jac_blocks, jac_rows, jac_cols, landing, covariance_root):
    nnz, block, _ = jac_blocks.shape
    state_rows, mode_columns = covariance_root.shape
    nblk = state_rows // block
    rim = landing.shape[0] // 4
    slot_count = nblk + 4 * rim
    blocks = covariance_root.reshape(nblk, block, mode_columns)
    base, to_prev_x, to_next_x, to_prev_y, to_next_y = apply_blocks(
        jac_rows, jac_cols, jac_blocks, blocks, slot_count)
    from_next_x = shifted(to_prev_x, "tx", -1)
    from_prev_x = shifted(to_next_x, "tx", 1)
    from_next_y = shifted(to_prev_y, "ty", -1)
    from_prev_y = shifted(to_next_y, "ty", 1)
    predicted_root, local_tiles = land_and_gram(
        landing, base, [from_next_x, from_prev_x, from_next_y, from_prev_y])
    total_rows = state_rows * lax.axis_size("tx") * lax.axis_size("ty")
    tiles = mode_columns // block
    upper_sum = grouped_sum(local_tiles.reshape(-1, block)).reshape(local_tiles.shape)
    rescaled_orthogonal_root, r_factor = factor_solve(upper_sum, predicted_root, total_rows, block)
    return (rescaled_orthogonal_root, r_factor)


def solution(mesh):
    placed = (
        P(("basin", "tx", "ty"), None, None),
        P(("basin", "tx", "ty")),
        P(("basin", "tx", "ty")),
        P(("basin", "tx", "ty")),
        P(("basin", "tx", "ty"), None),
    )
    return jax.shard_map(
        per_device,
        mesh=mesh,
        in_specs=placed,
        out_specs=(P(("basin", "tx", "ty"), None), P("basin", None)),
        check_vma=False,
    )
```
